256 devices in a mesh: section: 4 (over x_hi, core), seq: 64 (over y, x_lo, z).
Axes of the slice: x: 4 (x_hi: 2, x_lo: 2; x = x_hi * 2 + x_lo), y: 4, z: 8, core: 2. Of those that a mesh axis runs over, the one named last changes fastest.
Arguments:
- activations: bfloat16 [4, 16384, 1024], P('section', 'seq'), may hold values from -54 to 54
- cotangent: bfloat16 [4, 16384, 1024], P('section', 'seq'), may hold values from -6 to 6
- input_weights: bfloat16 [4, 1024, 3072], P('section'), may hold values from -3 to 3
- output_weights: bfloat16 [4, 1024, 1024], P('section'), may hold values from -0.1875 to 0.1875
- key_blocks: int32 [128, 4], P('seq'), may hold values from 0 to 127, as said below
- block_counts: int32 [128], P('seq'), may hold values from 1 to 4, as said below
Outputs:
- forward_out: bfloat16 [4, 16384, 1024], P('section', 'seq')
- backward_out: bfloat16 [4, 16384, 1024], P('section', 'seq')
The draws below stay inside these ranges and needn't reach their ends.
Inputs may be any that keep to these rules, and one draw needn't show every extreme that they name: `key_blocks`: row b: slot 0 is b; slots 1 to block_counts[b] - 1 hold distinct blocks other than b, at most 2 blocks from b; later slots repeat b. `block_counts`: some block has 4 live slots and some has 1.
All inputs are finite; a program needn't handle non-finite values.
Results may differ from the reference program's by a relative error of at most 0.0036.
Values may be sent and summed in bfloat16 or wider, within the bound.
No kernel may reach another device: no remote copies, remote signals or barrier semaphores. Data moves between devices by JAX's collectives and lax.ppermute only.
A program may use at most 128 MiB of HBM per device.

```python
import math
import jax
import jax.numpy as jnp
from jax import lax

D = 1024
HEADS = 8
HEAD_DIM = 128
BLOCK = 128
SLOTS = 4
REACH = 2
TOKENS = 16384
WIDTH = 1024
N_SECTION = 4


def draw_activations(key, part):
    base_key, row_key, column_key = jax.random.split(key, 3)
    shape = (N_SECTION, TOKENS, D)
    row_scale = jnp.exp(jax.random.uniform(row_key, (N_SECTION, TOKENS, 1), minval=math.log(0.3), maxval=math.log(3.0)))
    column_scale = jnp.exp(jax.random.uniform(column_key, (N_SECTION, 1, D), minval=math.log(0.3), maxval=math.log(3.0)))
    base = jnp.clip(jax.random.normal(base_key, shape), -6.0, 6.0)
    return (base * row_scale * column_scale).astype(jnp.bfloat16)


def draw_input_weights(key, part):
    base_key = jax.random.fold_in(key, 0)
    width = HEADS * HEAD_DIM
    base = jnp.clip(jax.random.normal(base_key, (N_SECTION, D, 3 * width)), -6.0, 6.0) / math.sqrt(D)
    return base.astype(jnp.bfloat16)


def neighbour_lists(key):
    order_key, count_key, full_key, single_key = jax.random.split(jax.random.fold_in(key, 11), 4)
    nblock = TOKENS // BLOCK
    offsets = jnp.concatenate([jnp.arange(-REACH, 0), jnp.arange(1, REACH + 1)]).astype(jnp.int32)
    blocks = jnp.arange(nblock, dtype=jnp.int32)
    candidates = blocks[:, None] + offsets[None, :]
    inside = (candidates >= 0) & (candidates < nblock)
    ranking = jax.random.randint(order_key, (nblock, 2 * REACH), 0, 1 << 20) * (2 * REACH) + jnp.arange(2 * REACH, dtype=jnp.int32)[None, :]
    ranking = jnp.where(inside, ranking, ranking + (1 << 26))
    ranked_order = jnp.argsort(ranking, axis=1)
    chosen = jnp.take_along_axis(candidates, ranked_order, axis=1)[:, :SLOTS - 1]
    counts = jax.random.randint(count_key, (nblock,), 1, SLOTS + 1)
    counts = jnp.minimum(counts, 1 + jnp.sum(inside.astype(jnp.int32), axis=1))
    full_block = jax.random.randint(full_key, (), REACH, nblock - REACH)
    single_block = jax.random.randint(single_key, (), 0, REACH)
    counts = jnp.where(blocks == full_block, SLOTS, counts)
    counts = jnp.where(blocks == single_block, 1, counts)
    block_lists = jnp.concatenate([blocks[:, None], chosen], axis=1)
    live_slots = jnp.arange(SLOTS, dtype=jnp.int32)[None, :] < counts[:, None]
    block_lists = jnp.where(live_slots, block_lists, blocks[:, None])
    return (block_lists.astype(jnp.int32), counts.astype(jnp.int32))


def draw_key_blocks(key, part):
    return neighbour_lists(key)[0]


def draw_block_counts(key, part):
    return neighbour_lists(key)[1]


def level_of(key, dims, shards, low, top_value):
    loudness, own = 1.0, jax.random.fold_in(key, 6)
    for dim, blocks in shards:
        heights = jnp.exp(jax.random.uniform(jax.random.fold_in(own, dim), (blocks,), jnp.float32, low / len(shards), top_value / len(shards)))
        loudness = loudness * jnp.repeat(heights, dims[dim] // blocks).reshape([-1 if axis == dim else 1 for axis in range(len(dims))])
    return loudness


def normal_values(key, dims, spread, bound, cuts=(), kind=jnp.bfloat16):
    drawn = spread * jax.random.normal(key, dims, jnp.float32)
    if cuts:
        drawn = drawn * level_of(key, dims, cuts, -0.22, 0.18)
    return jnp.clip(drawn, -bound, bound).astype(kind)


def setup_inputs(seed: int = 0) -> dict:
    seeds = jax.random.split(jax.random.key(seed), 7)
    activations = draw_activations(jax.random.fold_in(seeds[6], 71), 0)
    cotangent = normal_values(seeds[1], (N_SECTION, TOKENS, D), 1.0, 6.0, ((0, 4), (1, 64)))
    input_weights = draw_input_weights(jax.random.fold_in(seeds[6], 71), 0)
    output_weights = normal_values(seeds[3], (N_SECTION, WIDTH, D), WIDTH ** -0.5, 0.1875, ((0, 4),))
    key_blocks = draw_key_blocks(jax.random.fold_in(seeds[6], 71), 0)
    block_counts = draw_block_counts(jax.random.fold_in(seeds[6], 71), 0)
    return dict(activations=activations, cotangent=cotangent, input_weights=input_weights, output_weights=output_weights, key_blocks=key_blocks, block_counts=block_counts)


EPSILON = 1e-05

def rounded(values):
    return lax.optimization_barrier(values.astype(jnp.bfloat16)).astype(jnp.float32)

def section_layer(arrived, upstream, input_weights, output_weights, key_blocks, block_counts):
    exact = lax.Precision.HIGHEST
    nblock = key_blocks.shape[0]
    slot_count = key_blocks.shape[1]
    scaling = HEAD_DIM ** (-0.5)
    values = arrived.astype(jnp.float32)
    factor = lax.rsqrt(lax.optimization_barrier(jnp.mean(values * values, axis=-1, keepdims=True)) + EPSILON)
    normed = values * factor
    projected = rounded(jnp.dot(normed.astype(jnp.bfloat16), input_weights, preferred_element_type=jnp.float32))
    queries = projected[:, :WIDTH].reshape(nblock, BLOCK, HEADS, HEAD_DIM)
    key_value = projected[:, WIDTH:].reshape(nblock, BLOCK, 2 * WIDTH)
    picked = key_value[key_blocks]
    key_rows = picked[..., :WIDTH].reshape(nblock, slot_count, BLOCK, HEADS, HEAD_DIM)
    value_rows = picked[..., WIDTH:].reshape(nblock, slot_count, BLOCK, HEADS, HEAD_DIM)
    live_slots = (jnp.arange(slot_count)[None, :] < block_counts[:, None])[:, None, None, :, None]
    scores = jnp.einsum('bqhd,bskhd->bhqsk', queries, key_rows, precision=exact) * scaling
    scores = jnp.where(live_slots, scores, -1e+30)
    row_max = lax.optimization_barrier(jnp.max(scores, axis=(3, 4), keepdims=True))
    raw_weights = jnp.where(live_slots, jnp.exp(scores - row_max), 0.0)
    weights = raw_weights / lax.optimization_barrier(jnp.sum(raw_weights, axis=(3, 4), keepdims=True))
    weights_bf = rounded(weights)
    attended = jnp.einsum('bhqsk,bskhd->bqhd', weights_bf, value_rows, precision=exact).reshape(-1, WIDTH).astype(jnp.bfloat16)
    result = (values + jnp.dot(attended, output_weights, preferred_element_type=jnp.float32)).astype(jnp.bfloat16)
    attended_grad = rounded(jnp.dot(upstream, output_weights.T, preferred_element_type=jnp.float32))
    grad_blocks = attended_grad.reshape(nblock, BLOCK, HEADS, HEAD_DIM)
    weight_grad = jnp.einsum('bqhd,bskhd->bhqsk', grad_blocks, value_rows, precision=exact)
    weight_mean = lax.optimization_barrier(jnp.sum(weights * weight_grad, axis=(3, 4), keepdims=True))
    score_grad = rounded(weights * (weight_grad - weight_mean) * scaling)
    query_grad = jnp.einsum('bhqsk,bskhd->bqhd', score_grad, key_rows, precision=exact).reshape(-1, WIDTH)
    key_grad = jnp.einsum('bhqsk,bqhd->bskhd', score_grad, queries, precision=exact).reshape(nblock, slot_count, BLOCK, WIDTH)
    value_grad = jnp.einsum('bhqsk,bqhd->bskhd', weights_bf, grad_blocks, precision=exact).reshape(nblock, slot_count, BLOCK, WIDTH)
    grad_terms = jnp.concatenate([key_grad, value_grad], axis=-1)
    collected = jnp.zeros((nblock, BLOCK, 2 * WIDTH), jnp.float32).at[key_blocks].add(grad_terms)
    all_grads = jnp.concatenate([query_grad, collected.reshape(-1, 2 * WIDTH)], axis=-1).astype(jnp.bfloat16)
    normed_grad = jnp.dot(all_grads, input_weights.T, preferred_element_type=jnp.float32)
    correction = lax.optimization_barrier(jnp.mean(normed_grad * normed, axis=-1, keepdims=True))
    input_grad = (upstream.astype(jnp.float32) + factor * (normed_grad - normed * correction)).astype(jnp.bfloat16)
    return (result, input_grad)

def reference(activations, cotangent, input_weights, output_weights, key_blocks, block_counts):
    outputs = []
    gradients = []
    for section_index in range(N_SECTION):
        result, input_grad = section_layer(activations[(section_index - 1) % N_SECTION], cotangent[(section_index + 1) % N_SECTION], input_weights[section_index], output_weights[section_index], key_blocks, block_counts)
        outputs.append(result)
        gradients.append(input_grad)
    return (jnp.stack(outputs), jnp.stack(gradients))
```

```python
import functools

import jax
import jax.numpy as jnp
from jax import lax
from jax.experimental import pallas as pl
from jax.experimental.pallas import tpu as pltpu
from jax.sharding import PartitionSpec as P

HEAD_DIM = 128
BLOCK = 128
REACH = 2


EPSILON = 1e-05

NT = (((1,), (1,)), ((), ()))
TN = (((0,), (0,)), ((), ()))


def shifted(value, axis, steps):
    count = lax.axis_size(axis)
    pairs = [(source, (source + steps) % count) for source in range(count)]
    return lax.ppermute(value, axis, pairs)


def from_left(value, axis):
    count = lax.axis_size(axis)
    return lax.ppermute(value, axis, [(i, i + 1) for i in range(count - 1)])


def from_right(value, axis):
    count = lax.axis_size(axis)
    return lax.ppermute(value, axis, [(i + 1, i) for i in range(count - 1)])


def normalize(rows):
    values = rows.astype(jnp.float32)
    factor = lax.rsqrt(jnp.mean(values * values, axis=-1, keepdims=True) + EPSILON)
    return values, factor, values * factor


def attention_kernel(
    q_ref, ko_ref, vo_ref, kh_ref, vh_ref, do_ref, live_ref,
    out_ref, dq_ref, dk_ref, dv_ref, dkh_ref, dvh_ref,
):
    rows = q_ref.shape[0]
    margin = kh_ref.shape[0] // 2
    scaling = HEAD_DIM ** (-0.5)
    queries = q_ref[...]
    keys = jnp.concatenate([kh_ref[:margin], ko_ref[...], kh_ref[margin:]], axis=0)
    values = jnp.concatenate([vh_ref[:margin], vo_ref[...], vh_ref[margin:]], axis=0)
    grad_out = do_ref[...]
    live = live_ref[...] > 0
    scores = lax.dot_general(queries, keys, NT, preferred_element_type=jnp.float32) * scaling
    scores = jnp.where(live, scores, -1e30)
    row_max = jnp.max(scores, axis=1, keepdims=True)
    raw = jnp.where(live, jnp.exp(scores - row_max), 0.0)
    weights = raw / jnp.sum(raw, axis=1, keepdims=True)
    weights_bf = weights.astype(jnp.bfloat16)
    out_ref[...] = jnp.dot(weights_bf, values, preferred_element_type=jnp.float32).astype(
        out_ref.dtype
    )
    weight_grad = lax.dot_general(grad_out, values, NT, preferred_element_type=jnp.float32)
    weight_mean = jnp.sum(weights * weight_grad, axis=1, keepdims=True)
    score_grad = (weights * (weight_grad - weight_mean) * scaling).astype(jnp.bfloat16)
    dq_ref[...] = jnp.dot(score_grad, keys, preferred_element_type=jnp.float32).astype(dq_ref.dtype)
    key_grad = lax.dot_general(score_grad, queries, TN, preferred_element_type=jnp.float32)
    value_grad = lax.dot_general(weights_bf, grad_out, TN, preferred_element_type=jnp.float32)
    dtype = dk_ref.dtype
    dk_ref[...] = key_grad[margin : margin + rows].astype(dtype)
    dv_ref[...] = value_grad[margin : margin + rows].astype(dtype)
    dkh_ref[:margin] = key_grad[:margin].astype(dtype)
    dkh_ref[margin:] = key_grad[margin + rows :].astype(dtype)
    dvh_ref[:margin] = value_grad[:margin].astype(dtype)
    dvh_ref[margin:] = value_grad[margin + rows :].astype(dtype)


def attention(projected, halo_kv, attended_grad, live):
    rows, width = attended_grad.shape
    heads = width // HEAD_DIM
    halo_rows = halo_kv.shape[0]
    window = live.shape[1]
    own = lambda offset: pl.BlockSpec((rows, HEAD_DIM), lambda h: (0, offset + h))
    side = lambda offset: pl.BlockSpec((halo_rows, HEAD_DIM), lambda h: (0, offset + h))
    flops = heads * 5 * 2 * rows * window * HEAD_DIM
    moved = 2 * (2 * projected.size + 2 * halo_kv.size + 2 * attended_grad.size) + 4 * live.size
    own_shape = jax.ShapeDtypeStruct((rows, width), jnp.bfloat16)
    side_shape = jax.ShapeDtypeStruct((halo_rows, width), jnp.bfloat16)
    return pl.pallas_call(
        attention_kernel,
        grid=(heads,),
        in_specs=[
            own(0),
            own(heads),
            own(2 * heads),
            side(0),
            side(heads),
            own(0),
            pl.BlockSpec((rows, window), lambda h: (0, 0)),
        ],
        out_specs=[own(0), own(0), own(0), own(0), side(0), side(0)],
        out_shape=[own_shape, own_shape, own_shape, own_shape, side_shape, side_shape],
        compiler_params=pltpu.CompilerParams(dimension_semantics=("arbitrary",)),
        cost_estimate=pl.CostEstimate(
            flops=flops, transcendentals=heads * rows * window, bytes_accessed=moved
        ),
    )(projected, projected, projected, halo_kv, halo_kv, attended_grad, live)


def per_device(activations, cotangent, input_weights, output_weights, key_blocks, block_counts):
    arrived = shifted(activations[0], "section", 1)
    upstream = shifted(cotangent[0], "section", -1)
    weights_in = input_weights[0]
    weights_out = output_weights[0]
    width = weights_out.shape[0]
    rows = arrived.shape[0]
    nblock = rows // BLOCK
    slot_count = key_blocks.shape[1]
    margin = REACH * BLOCK
    assert margin <= rows
    span_blocks = nblock + 2 * REACH
    first_block = lax.axis_index("seq") * nblock

    halo_rows = jnp.concatenate(
        [from_left(arrived[rows - margin :], "seq"), from_right(arrived[:margin], "seq")], axis=0
    )
    values, factor, normed = normalize(arrived)
    projected = jnp.dot(
        normed.astype(jnp.bfloat16), weights_in, preferred_element_type=jnp.float32
    ).astype(jnp.bfloat16)
    attended_grad = jnp.einsum(
        "rd,wd->rw", upstream, weights_out, preferred_element_type=jnp.float32
    ).astype(jnp.bfloat16)
    _, _, halo_normed = normalize(halo_rows)
    weights_kv = weights_in[:, width:]
    halo_kv = jnp.dot(
        halo_normed.astype(jnp.bfloat16), weights_kv, preferred_element_type=jnp.float32
    ).astype(jnp.bfloat16)

    window_index = key_blocks - first_block + REACH
    live_slots = jnp.arange(slot_count)[None, :] < block_counts[:, None]
    live_blocks = jnp.any(
        live_slots[:, :, None] & (window_index[:, :, None] == jnp.arange(span_blocks)[None, None, :]),
        axis=1,
    )
    live = jnp.repeat(jnp.repeat(live_blocks, BLOCK, axis=0), BLOCK, axis=1).astype(jnp.float32)

    attended, query_grad, key_grad, value_grad, halo_key_grad, halo_value_grad = attention(
        projected, halo_kv, attended_grad, live
    )
    result = (values + jnp.dot(attended, weights_out, preferred_element_type=jnp.float32)).astype(
        jnp.bfloat16
    )

    halo_grads = jnp.concatenate([halo_key_grad, halo_value_grad], axis=1)
    halo_normed_grad = jnp.einsum(
        "rc,dc->rd", halo_grads, weights_kv, preferred_element_type=jnp.float32
    ).astype(jnp.bfloat16)
    head_part = from_left(halo_normed_grad[margin:], "seq")
    tail_part = from_right(halo_normed_grad[:margin], "seq")
    own_grads = jnp.concatenate([query_grad, key_grad, value_grad], axis=1)
    normed_grad = jnp.einsum("rc,dc->rd", own_grads, weights_in, preferred_element_type=jnp.float32)
    normed_grad = normed_grad + jnp.pad(head_part.astype(jnp.float32), ((0, rows - margin), (0, 0)))
    normed_grad = normed_grad + jnp.pad(tail_part.astype(jnp.float32), ((rows - margin, 0), (0, 0)))
    correction = jnp.mean(normed_grad * normed, axis=-1, keepdims=True)
    input_grad = (
        upstream.astype(jnp.float32) + factor * (normed_grad - normed * correction)
    ).astype(jnp.bfloat16)
    return (result[None], input_grad[None])


def solution(mesh):
    in_specs = (
        P("section", "seq", None),
        P("section", "seq", None),
        P("section", None, None),
        P("section", None, None),
        P("seq", None),
        P("seq"),
    )
    out_specs = (P("section", "seq", None), P("section", "seq", None))
    return jax.shard_map(
        per_device, mesh=mesh, in_specs=in_specs, out_specs=out_specs, check_vma=False
    )
```

```python
import functools

import jax
import jax.numpy as jnp
from jax import lax
from jax.experimental import pallas as pl
from jax.experimental.pallas import tpu as pltpu
from jax.sharding import PartitionSpec as P

HEAD_DIM = 128
BLOCK = 128
REACH = 2


EPSILON = 1e-05

NT = (((1,), (1,)), ((), ()))
TN = (((0,), (0,)), ((), ()))


def shifted(value, axis, steps):
    count = lax.axis_size(axis)
    pairs = [(source, (source + steps) % count) for source in range(count)]
    return lax.ppermute(value, axis, pairs)


def from_left(value, axis):
    count = lax.axis_size(axis)
    return lax.ppermute(value, axis, [(i, i + 1) for i in range(count - 1)])


def from_right(value, axis):
    count = lax.axis_size(axis)
    return lax.ppermute(value, axis, [(i + 1, i) for i in range(count - 1)])


def normalize(rows):
    values = rows.astype(jnp.float32)
    factor = lax.rsqrt(jnp.mean(values * values, axis=-1, keepdims=True) + EPSILON)
    return values, factor, values * factor


def attention_kernel(
    q_ref, ko_ref, vo_ref, kh_ref, vh_ref, do_ref, live_ref,
    out_ref, dq_ref, dk_ref, dv_ref, dkh_ref, dvh_ref,
):
    rows = q_ref.shape[0]
    margin = kh_ref.shape[0] // 2
    scaling = HEAD_DIM ** (-0.5)
    queries = q_ref[...]
    keys = jnp.concatenate([kh_ref[:margin], ko_ref[...], kh_ref[margin:]], axis=0)
    values = jnp.concatenate([vh_ref[:margin], vo_ref[...], vh_ref[margin:]], axis=0)
    grad_out = do_ref[...]
    scores = lax.dot_general(queries, keys, NT, preferred_element_type=jnp.float32) * scaling
    scores = scores + live_ref[...]
    row_max = jnp.max(scores, axis=1, keepdims=True)
    raw = jnp.exp(scores - row_max)
    weights = raw * (1.0 / jnp.sum(raw, axis=1, keepdims=True))
    weights_bf = weights.astype(jnp.bfloat16)
    out_ref[...] = jnp.dot(weights_bf, values, preferred_element_type=jnp.float32).astype(
        out_ref.dtype
    )
    weight_grad = lax.dot_general(grad_out, values, NT, preferred_element_type=jnp.float32)
    weight_mean = jnp.sum(weights * weight_grad, axis=1, keepdims=True)
    score_grad = (weights * (weight_grad - weight_mean) * scaling).astype(jnp.bfloat16)
    dq_ref[...] = jnp.dot(score_grad, keys, preferred_element_type=jnp.float32).astype(dq_ref.dtype)
    key_grad = lax.dot_general(score_grad, queries, TN, preferred_element_type=jnp.float32)
    value_grad = lax.dot_general(weights_bf, grad_out, TN, preferred_element_type=jnp.float32)
    dtype = dk_ref.dtype
    dk_ref[...] = key_grad[margin : margin + rows].astype(dtype)
    dv_ref[...] = value_grad[margin : margin + rows].astype(dtype)
    dkh_ref[:margin] = key_grad[:margin].astype(dtype)
    dkh_ref[margin:] = key_grad[margin + rows :].astype(dtype)
    dvh_ref[:margin] = value_grad[:margin].astype(dtype)
    dvh_ref[margin:] = value_grad[margin + rows :].astype(dtype)


def attention(projected, halo_kv, attended_grad, live):
    rows, width = attended_grad.shape
    heads = width // HEAD_DIM
    halo_rows = halo_kv.shape[0]
    window = live.shape[1]
    own = lambda offset: pl.BlockSpec((rows, HEAD_DIM), lambda h: (0, offset + h))
    side = lambda offset: pl.BlockSpec((halo_rows, HEAD_DIM), lambda h: (0, offset + h))
    flops = heads * 5 * 2 * rows * window * HEAD_DIM
    moved = 2 * (2 * projected.size + 2 * halo_kv.size + 2 * attended_grad.size) + 4 * live.size
    own_shape = jax.ShapeDtypeStruct((rows, width), jnp.bfloat16)
    side_shape = jax.ShapeDtypeStruct((halo_rows, width), jnp.bfloat16)
    return pl.pallas_call(
        attention_kernel,
        grid=(heads,),
        in_specs=[
            own(0),
            own(heads),
            own(2 * heads),
            side(0),
            side(heads),
            own(0),
            pl.BlockSpec((rows, window), lambda h: (0, 0)),
        ],
        out_specs=[own(0), own(0), own(0), own(0), side(0), side(0)],
        out_shape=[own_shape, own_shape, own_shape, own_shape, side_shape, side_shape],
        compiler_params=pltpu.CompilerParams(dimension_semantics=("arbitrary",)),
        cost_estimate=pl.CostEstimate(
            flops=flops, transcendentals=heads * rows * window, bytes_accessed=moved
        ),
    )(projected, projected, projected, halo_kv, halo_kv, attended_grad, live)


def per_device(activations, cotangent, input_weights, output_weights, key_blocks, block_counts):
    arrived = shifted(activations[0], "section", 1)
    upstream = shifted(cotangent[0], "section", -1)
    weights_in = input_weights[0]
    weights_out = output_weights[0]
    width = weights_out.shape[0]
    rows = arrived.shape[0]
    nblock = rows // BLOCK
    slot_count = key_blocks.shape[1]
    margin = REACH * BLOCK
    assert margin <= rows
    span_blocks = nblock + 2 * REACH
    first_block = lax.axis_index("seq") * nblock

    halo_rows = jnp.concatenate(
        [from_left(arrived[rows - margin :], "seq"), from_right(arrived[:margin], "seq")], axis=0
    )
    values, factor, normed = normalize(arrived)
    projected = jnp.dot(
        normed.astype(jnp.bfloat16), weights_in, preferred_element_type=jnp.float32
    ).astype(jnp.bfloat16)
    attended_grad = jnp.einsum(
        "rd,wd->rw", upstream, weights_out, preferred_element_type=jnp.float32
    ).astype(jnp.bfloat16)
    _, _, halo_normed = normalize(halo_rows)
    weights_kv = weights_in[:, width:]
    halo_kv = jnp.dot(
        halo_normed.astype(jnp.bfloat16), weights_kv, preferred_element_type=jnp.float32
    ).astype(jnp.bfloat16)

    window_index = key_blocks - first_block + REACH
    live_slots = jnp.arange(slot_count)[None, :] < block_counts[:, None]
    live_blocks = jnp.any(
        live_slots[:, :, None] & (window_index[:, :, None] == jnp.arange(span_blocks)[None, None, :]),
        axis=1,
    )
    live = jnp.where(jnp.repeat(jnp.repeat(live_blocks, BLOCK, axis=0), BLOCK, axis=1), 0.0, -1e30)

    attended, query_grad, key_grad, value_grad, halo_key_grad, halo_value_grad = attention(
        projected, halo_kv, attended_grad, live
    )
    result = (values + jnp.dot(attended, weights_out, preferred_element_type=jnp.float32)).astype(
        jnp.bfloat16
    )

    halo_grads = jnp.concatenate([halo_key_grad, halo_value_grad], axis=1)
    halo_normed_grad = jnp.einsum(
        "rc,dc->rd", halo_grads, weights_kv, preferred_element_type=jnp.float32
    ).astype(jnp.bfloat16)
    head_part = from_left(halo_normed_grad[margin:], "seq")
    tail_part = from_right(halo_normed_grad[:margin], "seq")
    own_grads = jnp.concatenate([query_grad, key_grad, value_grad], axis=1)
    normed_grad = lax.optimization_barrier(
        jnp.einsum("rc,dc->rd", own_grads, weights_in, preferred_element_type=jnp.float32)
    )
    normed_grad = normed_grad + jnp.pad(head_part.astype(jnp.float32), ((0, rows - margin), (0, 0)))
    normed_grad = normed_grad + jnp.pad(tail_part.astype(jnp.float32), ((rows - margin, 0), (0, 0)))
    correction = jnp.mean(normed_grad * normed, axis=-1, keepdims=True)
    input_grad = (
        upstream.astype(jnp.float32) + factor * (normed_grad - normed * correction)
    ).astype(jnp.bfloat16)
    return (result[None], input_grad[None])


def solution(mesh):
    in_specs = (
        P("section", "seq", None),
        P("section", "seq", None),
        P("section", None, None),
        P("section", None, None),
        P("seq", None),
        P("seq"),
    )
    out_specs = (P("section", "seq", None), P("section", "seq", None))
    return jax.shard_map(
        per_device, mesh=mesh, in_specs=in_specs, out_specs=out_specs, check_vma=False
    )
```

```python
import functools

import jax
import jax.numpy as jnp
from jax import lax
from jax.experimental import pallas as pl
from jax.experimental.pallas import tpu as pltpu
from jax.sharding import PartitionSpec as P

HEAD_DIM = 128
BLOCK = 128
REACH = 2


EPSILON = 1e-05

NT = (((1,), (1,)), ((), ()))
TN = (((0,), (0,)), ((), ()))


def shifted(value, axis, steps):
    count = lax.axis_size(axis)
    pairs = [(source, (source + steps) % count) for source in range(count)]
    return lax.ppermute(value, axis, pairs)


def from_left(value, axis):
    count = lax.axis_size(axis)
    return lax.ppermute(value, axis, [(i, i + 1) for i in range(count - 1)])


def from_right(value, axis):
    count = lax.axis_size(axis)
    return lax.ppermute(value, axis, [(i + 1, i) for i in range(count - 1)])


def normalize(rows):
    values = rows.astype(jnp.float32)
    factor = lax.rsqrt(jnp.mean(values * values, axis=-1, keepdims=True) + EPSILON)
    return values, factor, values * factor


def attention_kernel(
    q_ref, ko_ref, vo_ref, kh_ref, vh_ref, do_ref, live_ref,
    out_ref, dq_ref, dk_ref, dv_ref, dkh_ref, dvh_ref,
):
    rows = q_ref.shape[0]
    margin = kh_ref.shape[0] // 2
    scaling = HEAD_DIM ** (-0.5)
    queries = q_ref[...]
    keys = jnp.concatenate([kh_ref[:margin], ko_ref[...], kh_ref[margin:]], axis=0)
    values = jnp.concatenate([vh_ref[:margin], vo_ref[...], vh_ref[margin:]], axis=0)
    grad_out = do_ref[...]
    scores = lax.dot_general(queries, keys, NT, preferred_element_type=jnp.float32) * scaling
    scores = scores + live_ref[...]
    row_max = jnp.max(scores, axis=1, keepdims=True)
    raw = jnp.exp(scores - row_max)
    weights = raw * (1.0 / jnp.sum(raw, axis=1, keepdims=True))
    weights_bf = weights.astype(jnp.bfloat16)
    out_ref[...] = jnp.dot(weights_bf, values, preferred_element_type=jnp.float32).astype(
        out_ref.dtype
    )
    weight_grad = lax.dot_general(grad_out, values, NT, preferred_element_type=jnp.float32)
    weight_mean = jnp.sum(weights * weight_grad, axis=1, keepdims=True)
    score_grad = (weights * (weight_grad - weight_mean) * scaling).astype(jnp.bfloat16)
    dq_ref[...] = jnp.dot(score_grad, keys, preferred_element_type=jnp.float32).astype(dq_ref.dtype)
    key_grad = lax.dot_general(score_grad, queries, TN, preferred_element_type=jnp.float32)
    value_grad = lax.dot_general(weights_bf, grad_out, TN, preferred_element_type=jnp.float32)
    dtype = dk_ref.dtype
    dk_ref[...] = key_grad[margin : margin + rows].astype(dtype)
    dv_ref[...] = value_grad[margin : margin + rows].astype(dtype)
    dkh_ref[:margin] = key_grad[:margin].astype(dtype)
    dkh_ref[margin:] = key_grad[margin + rows :].astype(dtype)
    dvh_ref[:margin] = value_grad[:margin].astype(dtype)
    dvh_ref[margin:] = value_grad[margin + rows :].astype(dtype)


def attention(projected, halo_kv, attended_grad, live):
    rows, width = attended_grad.shape
    heads = width // HEAD_DIM
    halo_rows = halo_kv.shape[0]
    window = live.shape[1]
    own = lambda offset: pl.BlockSpec((rows, HEAD_DIM), lambda h: (0, offset + h))
    side = lambda offset: pl.BlockSpec((halo_rows, HEAD_DIM), lambda h: (0, offset + h))
    flops = heads * 5 * 2 * rows * window * HEAD_DIM
    moved = 2 * (2 * projected.size + 2 * halo_kv.size + 2 * attended_grad.size) + 4 * live.size
    own_shape = jax.ShapeDtypeStruct((rows, width), jnp.bfloat16)
    side_shape = jax.ShapeDtypeStruct((halo_rows, width), jnp.bfloat16)
    return pl.pallas_call(
        attention_kernel,
        grid=(heads,),
        in_specs=[
            own(0),
            own(heads),
            own(2 * heads),
            side(0),
            side(heads),
            own(0),
            pl.BlockSpec((rows, window), lambda h: (0, 0)),
        ],
        out_specs=[own(0), own(0), own(0), own(0), side(0), side(0)],
        out_shape=[own_shape, own_shape, own_shape, own_shape, side_shape, side_shape],
        compiler_params=pltpu.CompilerParams(dimension_semantics=("arbitrary",)),
        cost_estimate=pl.CostEstimate(
            flops=flops, transcendentals=heads * rows * window, bytes_accessed=moved
        ),
    )(projected, projected, projected, halo_kv, halo_kv, attended_grad, live)


def per_device(activations, cotangent, input_weights, output_weights, key_blocks, block_counts):
    arrived = shifted(activations[0], "section", 1)
    upstream = shifted(cotangent[0], "section", -1)
    weights_in = input_weights[0]
    weights_out = output_weights[0]
    width = weights_out.shape[0]
    rows = arrived.shape[0]
    nblock = rows // BLOCK
    slot_count = key_blocks.shape[1]
    margin = REACH * BLOCK
    assert margin <= rows
    span_blocks = nblock + 2 * REACH
    first_block = lax.axis_index("seq") * nblock

    halo_rows = jnp.concatenate(
        [from_left(arrived[rows - margin :], "seq"), from_right(arrived[:margin], "seq")], axis=0
    )
    values, factor, normed = normalize(arrived)
    projected = jnp.dot(
        lax.optimization_barrier(normed.astype(jnp.bfloat16)),
        weights_in,
        preferred_element_type=jnp.float32,
    ).astype(jnp.bfloat16)
    attended_grad = jnp.einsum(
        "rd,wd->rw", upstream, weights_out, preferred_element_type=jnp.float32
    ).astype(jnp.bfloat16)
    _, _, halo_normed = normalize(halo_rows)
    weights_kv = weights_in[:, width:]
    halo_kv = jnp.dot(
        lax.optimization_barrier(halo_normed.astype(jnp.bfloat16)),
        weights_kv,
        preferred_element_type=jnp.float32,
    ).astype(jnp.bfloat16)

    window_index = key_blocks - first_block + REACH
    live_slots = jnp.arange(slot_count)[None, :] < block_counts[:, None]
    live_blocks = jnp.any(
        live_slots[:, :, None] & (window_index[:, :, None] == jnp.arange(span_blocks)[None, None, :]),
        axis=1,
    )
    live = jnp.where(jnp.repeat(jnp.repeat(live_blocks, BLOCK, axis=0), BLOCK, axis=1), 0.0, -1e30)

    attended, query_grad, key_grad, value_grad, halo_key_grad, halo_value_grad = attention(
        projected, halo_kv, attended_grad, live
    )
    result = (values + jnp.dot(attended, weights_out, preferred_element_type=jnp.float32)).astype(
        jnp.bfloat16
    )

    halo_grads = jnp.concatenate([halo_key_grad, halo_value_grad], axis=1)
    halo_normed_grad = jnp.einsum(
        "rc,dc->rd", halo_grads, weights_kv, preferred_element_type=jnp.float32
    ).astype(jnp.bfloat16)
    head_part = from_left(halo_normed_grad[margin:], "seq")
    tail_part = from_right(halo_normed_grad[:margin], "seq")
    own_grads = jnp.concatenate([query_grad, key_grad, value_grad], axis=1)
    normed_grad = lax.optimization_barrier(
        jnp.einsum("rc,dc->rd", own_grads, weights_in, preferred_element_type=jnp.float32)
    )
    normed_grad = normed_grad + jnp.pad(head_part.astype(jnp.float32), ((0, rows - margin), (0, 0)))
    normed_grad = normed_grad + jnp.pad(tail_part.astype(jnp.float32), ((rows - margin, 0), (0, 0)))
    correction = jnp.mean(normed_grad * normed, axis=-1, keepdims=True)
    input_grad = (
        upstream.astype(jnp.float32) + factor * (normed_grad - normed * correction)
    ).astype(jnp.bfloat16)
    return (result[None], input_grad[None])


def solution(mesh):
    in_specs = (
        P("section", "seq", None),
        P("section", "seq", None),
        P("section", None, None),
        P("section", None, None),
        P("seq", None),
        P("seq"),
    )
    out_specs = (P("section", "seq", None), P("section", "seq", None))
    return jax.shard_map(
        per_device, mesh=mesh, in_specs=in_specs, out_specs=out_specs, check_vma=False
    )
```

```python
import functools

import jax
import jax.numpy as jnp
from jax import lax
from jax.experimental import pallas as pl
from jax.experimental.pallas import tpu as pltpu
from jax.sharding import PartitionSpec as P

HEAD_DIM = 128
BLOCK = 128
REACH = 2


EPSILON = 1e-05

NT = (((1,), (1,)), ((), ()))
TN = (((0,), (0,)), ((), ()))


def shifted(value, axis, steps):
    count = lax.axis_size(axis)
    pairs = [(source, (source + steps) % count) for source in range(count)]
    return lax.ppermute(value, axis, pairs)


def from_left(value, axis):
    count = lax.axis_size(axis)
    return lax.ppermute(value, axis, [(i, i + 1) for i in range(count - 1)])


def from_right(value, axis):
    count = lax.axis_size(axis)
    return lax.ppermute(value, axis, [(i + 1, i) for i in range(count - 1)])


def normalize(rows):
    values = rows.astype(jnp.float32)
    factor = lax.rsqrt(jnp.mean(values * values, axis=-1, keepdims=True) + EPSILON)
    return values, factor, values * factor


def attention_kernel(
    slot_ref, q_ref, ko_ref, vo_ref, kh_ref, vh_ref, do_ref, bias_ref,
    out_ref, dq_ref, dk_ref, dv_ref, dkh_ref, dvh_ref,
    key_window, value_window, key_acc, value_acc,
):
    rows = q_ref.shape[0]
    margin = kh_ref.shape[0] // 2
    nblock, slot_count = slot_ref.shape
    scaling = HEAD_DIM ** (-0.5)
    key_window[:margin] = kh_ref[:margin]
    key_window[margin : margin + rows] = ko_ref[...]
    key_window[margin + rows :] = kh_ref[margin:]
    value_window[:margin] = vh_ref[:margin]
    value_window[margin : margin + rows] = vo_ref[...]
    value_window[margin + rows :] = vh_ref[margin:]
    key_acc[...] = jnp.zeros_like(key_acc)
    value_acc[...] = jnp.zeros_like(value_acc)
    for block in range(nblock):
        here = slice(block * BLOCK, (block + 1) * BLOCK)
        starts = [
            pl.multiple_of(slot_ref[block, slot] * BLOCK, BLOCK) for slot in range(slot_count)
        ]
        queries = q_ref[here]
        grad_out = do_ref[here]
        keys = jnp.concatenate([key_window[pl.ds(start, BLOCK)] for start in starts], axis=0)
        values = jnp.concatenate([value_window[pl.ds(start, BLOCK)] for start in starts], axis=0)
        scores = lax.dot_general(queries, keys, NT, preferred_element_type=jnp.float32) * scaling
        scores = scores + bias_ref[block : block + 1, :]
        row_max = jnp.max(scores, axis=1, keepdims=True)
        raw = jnp.exp(scores - row_max)
        weights = raw * (1.0 / jnp.sum(raw, axis=1, keepdims=True))
        weights_bf = weights.astype(jnp.bfloat16)
        out_ref[here] = jnp.dot(weights_bf, values, preferred_element_type=jnp.float32).astype(
            out_ref.dtype
        )
        weight_grad = lax.dot_general(grad_out, values, NT, preferred_element_type=jnp.float32)
        weight_mean = jnp.sum(weights * weight_grad, axis=1, keepdims=True)
        score_grad = (weights * (weight_grad - weight_mean) * scaling).astype(jnp.bfloat16)
        dq_ref[here] = jnp.dot(score_grad, keys, preferred_element_type=jnp.float32).astype(
            dq_ref.dtype
        )
        key_grad = lax.dot_general(score_grad, queries, TN, preferred_element_type=jnp.float32)
        value_grad = lax.dot_general(weights_bf, grad_out, TN, preferred_element_type=jnp.float32)
        for slot, start in enumerate(starts):
            part = slice(slot * BLOCK, (slot + 1) * BLOCK)
            key_acc[pl.ds(start, BLOCK)] += key_grad[part]
            value_acc[pl.ds(start, BLOCK)] += value_grad[part]
    dtype = dk_ref.dtype
    dk_ref[...] = key_acc[margin : margin + rows].astype(dtype)
    dv_ref[...] = value_acc[margin : margin + rows].astype(dtype)
    dkh_ref[:margin] = key_acc[:margin].astype(dtype)
    dkh_ref[margin:] = key_acc[margin + rows :].astype(dtype)
    dvh_ref[:margin] = value_acc[:margin].astype(dtype)
    dvh_ref[margin:] = value_acc[margin + rows :].astype(dtype)


def attention(projected, halo_kv, attended_grad, slot_window, slot_bias):
    rows, width = attended_grad.shape
    heads = width // HEAD_DIM
    halo_rows = halo_kv.shape[0]
    window_rows = rows + halo_rows
    nblock, slot_count = slot_window.shape
    keys = slot_count * BLOCK
    own = lambda offset: pl.BlockSpec((rows, HEAD_DIM), lambda h, s: (0, offset + h))
    side = lambda offset: pl.BlockSpec((halo_rows, HEAD_DIM), lambda h, s: (0, offset + h))
    flops = heads * 5 * 2 * rows * keys * HEAD_DIM
    moved = 2 * (2 * projected.size + 2 * halo_kv.size + 2 * attended_grad.size) + 4 * slot_bias.size
    own_shape = jax.ShapeDtypeStruct((rows, width), jnp.bfloat16)
    side_shape = jax.ShapeDtypeStruct((halo_rows, width), jnp.bfloat16)
    grid_spec = pltpu.PrefetchScalarGridSpec(
        num_scalar_prefetch=1,
        grid=(heads,),
        in_specs=[
            own(0),
            own(heads),
            own(2 * heads),
            side(0),
            side(heads),
            own(0),
            pl.BlockSpec((nblock, keys), lambda h, s: (0, 0)),
        ],
        out_specs=[own(0), own(0), own(0), own(0), side(0), side(0)],
        scratch_shapes=[
            pltpu.VMEM((window_rows, HEAD_DIM), jnp.bfloat16),
            pltpu.VMEM((window_rows, HEAD_DIM), jnp.bfloat16),
            pltpu.VMEM((window_rows, HEAD_DIM), jnp.float32),
            pltpu.VMEM((window_rows, HEAD_DIM), jnp.float32),
        ],
    )
    return pl.pallas_call(
        attention_kernel,
        grid_spec=grid_spec,
        out_shape=[own_shape, own_shape, own_shape, own_shape, side_shape, side_shape],
        compiler_params=pltpu.CompilerParams(dimension_semantics=("arbitrary",)),
        cost_estimate=pl.CostEstimate(
            flops=flops, transcendentals=heads * rows * keys, bytes_accessed=moved
        ),
    )(slot_window, projected, projected, projected, halo_kv, halo_kv, attended_grad, slot_bias)


def per_device(activations, cotangent, input_weights, output_weights, key_blocks, block_counts):
    arrived = shifted(activations[0], "section", 1)
    upstream = shifted(cotangent[0], "section", -1)
    weights_in = input_weights[0]
    weights_out = output_weights[0]
    width = weights_out.shape[0]
    rows = arrived.shape[0]
    nblock = rows // BLOCK
    slot_count = key_blocks.shape[1]
    margin = REACH * BLOCK
    assert margin <= rows
    span_blocks = nblock + 2 * REACH
    first_block = lax.axis_index("seq") * nblock

    halo_rows = jnp.concatenate(
        [from_left(arrived[rows - margin :], "seq"), from_right(arrived[:margin], "seq")], axis=0
    )
    values, factor, normed = normalize(arrived)
    projected = jnp.dot(
        lax.optimization_barrier(normed.astype(jnp.bfloat16)),
        weights_in,
        preferred_element_type=jnp.float32,
    ).astype(jnp.bfloat16)
    attended_grad = jnp.einsum(
        "rd,wd->rw", upstream, weights_out, preferred_element_type=jnp.float32
    ).astype(jnp.bfloat16)
    _, _, halo_normed = normalize(halo_rows)
    weights_kv = weights_in[:, width:]
    halo_kv = jnp.dot(
        lax.optimization_barrier(halo_normed.astype(jnp.bfloat16)),
        weights_kv,
        preferred_element_type=jnp.float32,
    ).astype(jnp.bfloat16)

    window_index = jnp.clip(key_blocks - first_block + REACH, 0, span_blocks - 1)
    live_slots = jnp.arange(slot_count)[None, :] < block_counts[:, None]
    slot_bias = jnp.repeat(jnp.where(live_slots, 0.0, -1e30), BLOCK, axis=1)

    attended, query_grad, key_grad, value_grad, halo_key_grad, halo_value_grad = attention(
        projected, halo_kv, attended_grad, window_index.astype(jnp.int32), slot_bias
    )
    result = (values + jnp.dot(attended, weights_out, preferred_element_type=jnp.float32)).astype(
        jnp.bfloat16
    )

    halo_grads = jnp.concatenate([halo_key_grad, halo_value_grad], axis=1)
    halo_normed_grad = jnp.einsum(
        "rc,dc->rd", halo_grads, weights_kv, preferred_element_type=jnp.float32
    ).astype(jnp.bfloat16)
    head_part = from_left(halo_normed_grad[margin:], "seq")
    tail_part = from_right(halo_normed_grad[:margin], "seq")
    own_grads = jnp.concatenate([query_grad, key_grad, value_grad], axis=1)
    normed_grad = lax.optimization_barrier(
        jnp.einsum("rc,dc->rd", own_grads, weights_in, preferred_element_type=jnp.float32)
    )
    normed_grad = normed_grad + jnp.pad(head_part.astype(jnp.float32), ((0, rows - margin), (0, 0)))
    normed_grad = normed_grad + jnp.pad(tail_part.astype(jnp.float32), ((rows - margin, 0), (0, 0)))
    correction = jnp.mean(normed_grad * normed, axis=-1, keepdims=True)
    input_grad = (
        upstream.astype(jnp.float32) + factor * (normed_grad - normed * correction)
    ).astype(jnp.bfloat16)
    return (result[None], input_grad[None])


def solution(mesh):
    in_specs = (
        P("section", "seq", None),
        P("section", "seq", None),
        P("section", None, None),
        P("section", None, None),
        P("seq", None),
        P("seq"),
    )
    out_specs = (P("section", "seq", None), P("section", "seq", None))
    return jax.shard_map(
        per_device, mesh=mesh, in_specs=in_specs, out_specs=out_specs, check_vma=False
    )
```

```python
import functools

import jax
import jax.numpy as jnp
from jax import lax
from jax.experimental import pallas as pl
from jax.experimental.pallas import tpu as pltpu
from jax.sharding import PartitionSpec as P

HEAD_DIM = 128
BLOCK = 128
REACH = 2


EPSILON = 1e-05

NT = (((1,), (1,)), ((), ()))
TN = (((0,), (0,)), ((), ()))


def shifted(value, axis, steps):
    count = lax.axis_size(axis)
    pairs = [(source, (source + steps) % count) for source in range(count)]
    return lax.ppermute(value, axis, pairs)


def from_left(value, axis):
    count = lax.axis_size(axis)
    return lax.ppermute(value, axis, [(i, i + 1) for i in range(count - 1)])


def from_right(value, axis):
    count = lax.axis_size(axis)
    return lax.ppermute(value, axis, [(i + 1, i) for i in range(count - 1)])


def normalize(rows):
    values = rows.astype(jnp.float32)
    factor = lax.rsqrt(jnp.mean(values * values, axis=-1, keepdims=True) + EPSILON)
    return values, factor, values * factor


def attention_kernel(
    q_ref, ko_ref, vo_ref, kh_ref, vh_ref, do_ref, live_ref, wk_ref, wv_ref,
    out_ref, dq_ref, dk_ref, dv_ref, halo_ref, halo_acc,
):
    head = pl.program_id(0)
    rows = q_ref.shape[0]
    margin = kh_ref.shape[0] // 2
    scaling = HEAD_DIM ** (-0.5)
    queries = q_ref[...]
    keys = jnp.concatenate([kh_ref[:margin], ko_ref[...], kh_ref[margin:]], axis=0)
    values = jnp.concatenate([vh_ref[:margin], vo_ref[...], vh_ref[margin:]], axis=0)
    grad_out = do_ref[...]
    scores = lax.dot_general(queries, keys, NT, preferred_element_type=jnp.float32) * scaling
    scores = scores + live_ref[...]
    row_max = jnp.max(scores, axis=1, keepdims=True)
    raw = jnp.exp(scores - row_max)
    weights = raw * (1.0 / jnp.sum(raw, axis=1, keepdims=True))
    weights_bf = weights.astype(jnp.bfloat16)
    out_ref[...] = jnp.dot(weights_bf, values, preferred_element_type=jnp.float32).astype(
        out_ref.dtype
    )
    weight_grad = lax.dot_general(grad_out, values, NT, preferred_element_type=jnp.float32)
    weight_mean = jnp.sum(weights * weight_grad, axis=1, keepdims=True)
    score_grad = (weights * (weight_grad - weight_mean) * scaling).astype(jnp.bfloat16)
    dq_ref[...] = jnp.dot(score_grad, keys, preferred_element_type=jnp.float32).astype(dq_ref.dtype)
    key_grad = lax.dot_general(score_grad, queries, TN, preferred_element_type=jnp.float32)
    value_grad = lax.dot_general(weights_bf, grad_out, TN, preferred_element_type=jnp.float32)
    dtype = dk_ref.dtype
    dk_ref[...] = key_grad[margin : margin + rows].astype(dtype)
    dv_ref[...] = value_grad[margin : margin + rows].astype(dtype)
    halo_key = jnp.concatenate([key_grad[:margin], key_grad[margin + rows :]], axis=0)
    halo_value = jnp.concatenate([value_grad[:margin], value_grad[margin + rows :]], axis=0)
    partial = lax.dot_general(
        halo_key.astype(dtype), wk_ref[...], NT, preferred_element_type=jnp.float32
    ) + lax.dot_general(
        halo_value.astype(dtype), wv_ref[...], NT, preferred_element_type=jnp.float32
    )

    @pl.when(head == 0)
    def _():
        halo_acc[...] = partial

    @pl.when(head > 0)
    def _():
        halo_acc[...] += partial

    @pl.when(head == pl.num_programs(0) - 1)
    def _():
        halo_ref[...] = halo_acc[...].astype(halo_ref.dtype)


def attention(projected, halo_kv, attended_grad, live, weights_in):
    rows, width = attended_grad.shape
    heads = width // HEAD_DIM
    halo_rows = halo_kv.shape[0]
    window = live.shape[1]
    own = lambda offset: pl.BlockSpec((rows, HEAD_DIM), lambda h: (0, offset + h))
    side = lambda offset: pl.BlockSpec((halo_rows, HEAD_DIM), lambda h: (0, offset + h))
    flops = heads * 5 * 2 * rows * window * HEAD_DIM
    moved = 2 * (2 * projected.size + 2 * halo_kv.size + 2 * attended_grad.size) + 4 * live.size
    own_shape = jax.ShapeDtypeStruct((rows, width), jnp.bfloat16)
    features = weights_in.shape[0]
    column = lambda offset: pl.BlockSpec((features, HEAD_DIM), lambda h: (0, offset + h))
    flops += heads * 2 * 2 * halo_rows * HEAD_DIM * features
    moved += 2 * 2 * features * width + 2 * halo_rows * features
    return pl.pallas_call(
        attention_kernel,
        grid=(heads,),
        in_specs=[
            own(0),
            own(heads),
            own(2 * heads),
            side(0),
            side(heads),
            own(0),
            pl.BlockSpec((rows, window), lambda h: (0, 0)),
            column(heads),
            column(2 * heads),
        ],
        out_specs=[
            own(0), own(0), own(0), own(0), pl.BlockSpec((halo_rows, features), lambda h: (0, 0))
        ],
        out_shape=[
            own_shape, own_shape, own_shape, own_shape,
            jax.ShapeDtypeStruct((halo_rows, features), jnp.bfloat16),
        ],
        scratch_shapes=[pltpu.VMEM((halo_rows, features), jnp.float32)],
        compiler_params=pltpu.CompilerParams(dimension_semantics=("arbitrary",)),
        cost_estimate=pl.CostEstimate(
            flops=flops, transcendentals=heads * rows * window, bytes_accessed=moved
        ),
    )(projected, projected, projected, halo_kv, halo_kv, attended_grad, live, weights_in, weights_in)


def per_device(activations, cotangent, input_weights, output_weights, key_blocks, block_counts):
    arrived = shifted(activations[0], "section", 1)
    upstream = shifted(cotangent[0], "section", -1)
    weights_in = input_weights[0]
    weights_out = output_weights[0]
    width = weights_out.shape[0]
    rows = arrived.shape[0]
    nblock = rows // BLOCK
    slot_count = key_blocks.shape[1]
    margin = REACH * BLOCK
    assert margin <= rows
    span_blocks = nblock + 2 * REACH
    first_block = lax.axis_index("seq") * nblock

    halo_rows = jnp.concatenate(
        [from_left(arrived[rows - margin :], "seq"), from_right(arrived[:margin], "seq")], axis=0
    )
    values, factor, normed = normalize(arrived)
    projected = jnp.dot(
        normed.astype(jnp.bfloat16), weights_in, preferred_element_type=jnp.float32
    ).astype(jnp.bfloat16)
    attended_grad = jnp.einsum(
        "rd,wd->rw", upstream, weights_out, preferred_element_type=jnp.float32
    ).astype(jnp.bfloat16)
    _, _, halo_normed = normalize(halo_rows)
    weights_kv = weights_in[:, width:]
    halo_kv = jnp.dot(
        halo_normed.astype(jnp.bfloat16), weights_kv, preferred_element_type=jnp.float32
    ).astype(jnp.bfloat16)

    window_index = key_blocks - first_block + REACH
    live_slots = jnp.arange(slot_count)[None, :] < block_counts[:, None]
    live_blocks = jnp.any(
        live_slots[:, :, None] & (window_index[:, :, None] == jnp.arange(span_blocks)[None, None, :]),
        axis=1,
    )
    live = jnp.where(jnp.repeat(jnp.repeat(live_blocks, BLOCK, axis=0), BLOCK, axis=1), 0.0, -1e30)

    attended, query_grad, key_grad, value_grad, halo_normed_grad = attention(
        projected, halo_kv, attended_grad, live, weights_in
    )
    result = (values + jnp.dot(attended, weights_out, preferred_element_type=jnp.float32)).astype(
        jnp.bfloat16
    )

    head_part = from_left(halo_normed_grad[margin:], "seq")
    tail_part = from_right(halo_normed_grad[:margin], "seq")
    own_grads = jnp.concatenate([query_grad, key_grad, value_grad], axis=1)
    normed_grad = lax.optimization_barrier(
        jnp.einsum("rc,dc->rd", own_grads, weights_in, preferred_element_type=jnp.float32)
    )
    normed_grad = normed_grad + jnp.pad(head_part.astype(jnp.float32), ((0, rows - margin), (0, 0)))
    normed_grad = normed_grad + jnp.pad(tail_part.astype(jnp.float32), ((rows - margin, 0), (0, 0)))
    correction = jnp.mean(normed_grad * normed, axis=-1, keepdims=True)
    input_grad = (
        upstream.astype(jnp.float32) + factor * (normed_grad - normed * correction)
    ).astype(jnp.bfloat16)
    return (result[None], input_grad[None])


def solution(mesh):
    in_specs = (
        P("section", "seq", None),
        P("section", "seq", None),
        P("section", None, None),
        P("section", None, None),
        P("seq", None),
        P("seq"),
    )
    out_specs = (P("section", "seq", None), P("section", "seq", None))
    return jax.shard_map(
        per_device, mesh=mesh, in_specs=in_specs, out_specs=out_specs, check_vma=False
    )
```

```python
import functools

import jax
import jax.numpy as jnp
from jax import lax
from jax.experimental import pallas as pl
from jax.experimental.pallas import tpu as pltpu
from jax.sharding import PartitionSpec as P

HEAD_DIM = 128
BLOCK = 128
REACH = 2


EPSILON = 1e-05

NT = (((1,), (1,)), ((), ()))
TN = (((0,), (0,)), ((), ()))


def shifted(value, axis, steps):
    count = lax.axis_size(axis)
    pairs = [(source, (source + steps) % count) for source in range(count)]
    return lax.ppermute(value, axis, pairs)


def from_left(value, axis):
    count = lax.axis_size(axis)
    return lax.ppermute(value, axis, [(i, i + 1) for i in range(count - 1)])


def from_right(value, axis):
    count = lax.axis_size(axis)
    return lax.ppermute(value, axis, [(i + 1, i) for i in range(count - 1)])


def grid_permute(value, moves):
    sections = lax.axis_size("section")
    count = lax.axis_size("seq")
    pairs = [
        (s * count + q, t * count + r)
        for s in range(0, sections, 2)
        for q in range(count)
        for t, r in [moves(s, q)]
        if 0 <= r < count
    ]
    return lax.ppermute(value, ("section", "seq"), pairs)


def halo_of(local, arrived, margin):
    rows = local.shape[0]
    if lax.axis_size("section") % 2:
        return jnp.concatenate(
            [from_left(arrived[rows - margin :], "seq"), from_right(arrived[:margin], "seq")], axis=0
        )
    left = grid_permute(local[rows - margin :], lambda s, q: (s + 1, q + 1)) + grid_permute(
        arrived[rows - margin :], lambda s, q: (s, q + 1)
    )
    right = grid_permute(local[:margin], lambda s, q: (s + 1, q - 1)) + grid_permute(
        arrived[:margin], lambda s, q: (s, q - 1)
    )
    return jnp.concatenate([left, right], axis=0)


def normalize(rows):
    values = rows.astype(jnp.float32)
    factor = lax.rsqrt(jnp.mean(values * values, axis=-1, keepdims=True) + EPSILON)
    return values, factor, values * factor


def attention_kernel(
    q_ref, ko_ref, vo_ref, kh_ref, vh_ref, do_ref, live_ref,
    out_ref, dq_ref, dk_ref, dv_ref, dkh_ref, dvh_ref,
):
    rows = q_ref.shape[0]
    margin = kh_ref.shape[0] // 2
    scaling = HEAD_DIM ** (-0.5)
    queries = q_ref[...]
    keys = jnp.concatenate([kh_ref[:margin], ko_ref[...], kh_ref[margin:]], axis=0)
    values = jnp.concatenate([vh_ref[:margin], vo_ref[...], vh_ref[margin:]], axis=0)
    grad_out = do_ref[...]
    scores = lax.dot_general(queries, keys, NT, preferred_element_type=jnp.float32) * scaling
    scores = scores + live_ref[...]
    row_max = jnp.max(scores, axis=1, keepdims=True)
    raw = jnp.exp(scores - row_max)
    weights = raw * (1.0 / jnp.sum(raw, axis=1, keepdims=True))
    weights_bf = weights.astype(jnp.bfloat16)
    out_ref[...] = jnp.dot(weights_bf, values, preferred_element_type=jnp.float32).astype(
        out_ref.dtype
    )
    weight_grad = lax.dot_general(grad_out, values, NT, preferred_element_type=jnp.float32)
    weight_mean = jnp.sum(weights * weight_grad, axis=1, keepdims=True)
    score_grad = (weights * (weight_grad - weight_mean) * scaling).astype(jnp.bfloat16)
    dq_ref[...] = jnp.dot(score_grad, keys, preferred_element_type=jnp.float32).astype(dq_ref.dtype)
    key_grad = lax.dot_general(score_grad, queries, TN, preferred_element_type=jnp.float32)
    value_grad = lax.dot_general(weights_bf, grad_out, TN, preferred_element_type=jnp.float32)
    dtype = dk_ref.dtype
    dk_ref[...] = key_grad[margin : margin + rows].astype(dtype)
    dv_ref[...] = value_grad[margin : margin + rows].astype(dtype)
    dkh_ref[:margin] = key_grad[:margin].astype(dtype)
    dkh_ref[margin:] = key_grad[margin + rows :].astype(dtype)
    dvh_ref[:margin] = value_grad[:margin].astype(dtype)
    dvh_ref[margin:] = value_grad[margin + rows :].astype(dtype)


def attention(projected, halo_kv, attended_grad, live):
    rows, width = attended_grad.shape
    heads = width // HEAD_DIM
    halo_rows = halo_kv.shape[0]
    window = live.shape[1]
    own = lambda offset: pl.BlockSpec((rows, HEAD_DIM), lambda h: (0, offset + h))
    side = lambda offset: pl.BlockSpec((halo_rows, HEAD_DIM), lambda h: (0, offset + h))
    flops = heads * 5 * 2 * rows * window * HEAD_DIM
    moved = 2 * (2 * projected.size + 2 * halo_kv.size + 2 * attended_grad.size) + 4 * live.size
    own_shape = jax.ShapeDtypeStruct((rows, width), jnp.bfloat16)
    side_shape = jax.ShapeDtypeStruct((halo_rows, width), jnp.bfloat16)
    return pl.pallas_call(
        attention_kernel,
        grid=(heads,),
        in_specs=[
            own(0),
            own(heads),
            own(2 * heads),
            side(0),
            side(heads),
            own(0),
            pl.BlockSpec((rows, window), lambda h: (0, 0)),
        ],
        out_specs=[own(0), own(0), own(0), own(0), side(0), side(0)],
        out_shape=[own_shape, own_shape, own_shape, own_shape, side_shape, side_shape],
        compiler_params=pltpu.CompilerParams(dimension_semantics=("arbitrary",)),
        cost_estimate=pl.CostEstimate(
            flops=flops, transcendentals=heads * rows * window, bytes_accessed=moved
        ),
    )(projected, projected, projected, halo_kv, halo_kv, attended_grad, live)


def per_device(activations, cotangent, input_weights, output_weights, key_blocks, block_counts):
    arrived = shifted(activations[0], "section", 1)
    upstream = shifted(cotangent[0], "section", -1)
    weights_in = input_weights[0]
    weights_out = output_weights[0]
    width = weights_out.shape[0]
    rows = arrived.shape[0]
    nblock = rows // BLOCK
    slot_count = key_blocks.shape[1]
    margin = REACH * BLOCK
    assert margin <= rows
    span_blocks = nblock + 2 * REACH
    first_block = lax.axis_index("seq") * nblock

    halo_rows = halo_of(activations[0], arrived, margin)
    values, factor, normed = normalize(arrived)
    projected = jnp.dot(
        normed.astype(jnp.bfloat16), weights_in, preferred_element_type=jnp.float32
    ).astype(jnp.bfloat16)
    attended_grad = jnp.einsum(
        "rd,wd->rw", upstream, weights_out, preferred_element_type=jnp.float32
    ).astype(jnp.bfloat16)
    _, _, halo_normed = normalize(halo_rows)
    weights_kv = weights_in[:, width:]
    halo_kv = jnp.dot(
        halo_normed.astype(jnp.bfloat16), weights_kv, preferred_element_type=jnp.float32
    ).astype(jnp.bfloat16)

    window_index = key_blocks - first_block + REACH
    live_slots = jnp.arange(slot_count)[None, :] < block_counts[:, None]
    live_blocks = jnp.any(
        live_slots[:, :, None] & (window_index[:, :, None] == jnp.arange(span_blocks)[None, None, :]),
        axis=1,
    )
    live = jnp.where(jnp.repeat(jnp.repeat(live_blocks, BLOCK, axis=0), BLOCK, axis=1), 0.0, -1e30)

    attended, query_grad, key_grad, value_grad, halo_key_grad, halo_value_grad = attention(
        projected, halo_kv, attended_grad, live
    )
    result = (values + jnp.dot(attended, weights_out, preferred_element_type=jnp.float32)).astype(
        jnp.bfloat16
    )

    halo_grads = jnp.concatenate([halo_key_grad, halo_value_grad], axis=1)
    halo_normed_grad = jnp.einsum(
        "rc,dc->rd", halo_grads, weights_kv, preferred_element_type=jnp.float32
    ).astype(jnp.bfloat16)
    head_part = from_left(halo_normed_grad[margin:], "seq")
    tail_part = from_right(halo_normed_grad[:margin], "seq")
    own_grads = jnp.concatenate([query_grad, key_grad, value_grad], axis=1)
    normed_grad = lax.optimization_barrier(
        jnp.einsum("rc,dc->rd", own_grads, weights_in, preferred_element_type=jnp.float32)
    )
    normed_grad = normed_grad + jnp.pad(head_part.astype(jnp.float32), ((0, rows - margin), (0, 0)))
    normed_grad = normed_grad + jnp.pad(tail_part.astype(jnp.float32), ((rows - margin, 0), (0, 0)))
    correction = jnp.mean(normed_grad * normed, axis=-1, keepdims=True)
    input_grad = (
        upstream.astype(jnp.float32) + factor * (normed_grad - normed * correction)
    ).astype(jnp.bfloat16)
    return (result[None], input_grad[None])


def solution(mesh):
    in_specs = (
        P("section", "seq", None),
        P("section", "seq", None),
        P("section", None, None),
        P("section", None, None),
        P("seq", None),
        P("seq"),
    )
    out_specs = (P("section", "seq", None), P("section", "seq", None))
    return jax.shard_map(
        per_device, mesh=mesh, in_specs=in_specs, out_specs=out_specs, check_vma=False
    )
```

```python
import functools

import jax
import jax.numpy as jnp
from jax import lax
from jax.experimental import pallas as pl
from jax.experimental.pallas import tpu as pltpu
from jax.sharding import PartitionSpec as P

HEAD_DIM = 128
BLOCK = 128
REACH = 2


EPSILON = 1e-05

NT = (((1,), (1,)), ((), ()))
TN = (((0,), (0,)), ((), ()))


def shifted(value, axis, steps):
    count = lax.axis_size(axis)
    pairs = [(source, (source + steps) % count) for source in range(count)]
    return lax.ppermute(value, axis, pairs)


def from_left(value, axis):
    count = lax.axis_size(axis)
    return lax.ppermute(value, axis, [(i, i + 1) for i in range(count - 1)])


def from_right(value, axis):
    count = lax.axis_size(axis)
    return lax.ppermute(value, axis, [(i + 1, i) for i in range(count - 1)])


def normalize(rows):
    values = rows.astype(jnp.float32)
    factor = lax.rsqrt(jnp.mean(values * values, axis=-1, keepdims=True) + EPSILON)
    return values, factor, values * factor


def attention_kernel(
    q_ref, ko_ref, vo_ref, kh_ref, vh_ref, do_ref, live_ref,
    out_ref, dq_ref, dk_ref, dv_ref, dkh_ref, dvh_ref,
):
    rows = q_ref.shape[0]
    margin = kh_ref.shape[0] // 2
    scaling = HEAD_DIM ** (-0.5)
    queries = q_ref[...]
    keys = jnp.concatenate([kh_ref[:margin], ko_ref[...], kh_ref[margin:]], axis=0)
    values = jnp.concatenate([vh_ref[:margin], vo_ref[...], vh_ref[margin:]], axis=0)
    grad_out = do_ref[...]
    scores = lax.dot_general(queries, keys, NT, preferred_element_type=jnp.float32) * scaling
    scores = scores + live_ref[...]
    row_max = jnp.max(scores, axis=1, keepdims=True)
    raw = jnp.exp(scores - row_max)
    weights = raw * (1.0 / jnp.sum(raw, axis=1, keepdims=True))
    weights_bf = weights.astype(jnp.bfloat16)
    out_ref[...] = jnp.dot(weights_bf, values, preferred_element_type=jnp.float32).astype(
        out_ref.dtype
    )
    weight_grad = lax.dot_general(grad_out, values, NT, preferred_element_type=jnp.float32)
    weight_mean = jnp.sum(weights * weight_grad, axis=1, keepdims=True)
    score_grad = (weights * (weight_grad - weight_mean) * scaling).astype(jnp.bfloat16)
    dq_ref[...] = jnp.dot(score_grad, keys, preferred_element_type=jnp.float32).astype(dq_ref.dtype)
    key_grad = lax.dot_general(score_grad, queries, TN, preferred_element_type=jnp.float32)
    value_grad = lax.dot_general(weights_bf, grad_out, TN, preferred_element_type=jnp.float32)
    dtype = dk_ref.dtype
    dk_ref[...] = key_grad[margin : margin + rows].astype(dtype)
    dv_ref[...] = value_grad[margin : margin + rows].astype(dtype)
    dkh_ref[:margin] = key_grad[:margin].astype(dtype)
    dkh_ref[margin:] = key_grad[margin + rows :].astype(dtype)
    dvh_ref[:margin] = value_grad[:margin].astype(dtype)
    dvh_ref[margin:] = value_grad[margin + rows :].astype(dtype)


def attention(projected, halo_kv, attended_grad, live):
    rows, width = attended_grad.shape
    heads = width // HEAD_DIM
    halo_rows = halo_kv.shape[0]
    window = live.shape[1]
    own = lambda offset: pl.BlockSpec((rows, HEAD_DIM), lambda h: (0, offset + h))
    side = lambda offset: pl.BlockSpec((halo_rows, HEAD_DIM), lambda h: (0, offset + h))
    flops = heads * 5 * 2 * rows * window * HEAD_DIM
    moved = 2 * (2 * projected.size + 2 * halo_kv.size + 2 * attended_grad.size) + 4 * live.size
    own_shape = jax.ShapeDtypeStruct((rows, width), jnp.bfloat16)
    side_shape = jax.ShapeDtypeStruct((halo_rows, width), jnp.bfloat16)
    return pl.pallas_call(
        attention_kernel,
        grid=(heads,),
        in_specs=[
            own(0),
            own(heads),
            own(2 * heads),
            side(0),
            side(heads),
            own(0),
            pl.BlockSpec((rows, window), lambda h: (0, 0)),
        ],
        out_specs=[own(0), own(0), own(0), own(0), side(0), side(0)],
        out_shape=[own_shape, own_shape, own_shape, own_shape, side_shape, side_shape],
        compiler_params=pltpu.CompilerParams(dimension_semantics=("arbitrary",)),
        cost_estimate=pl.CostEstimate(
            flops=flops, transcendentals=heads * rows * window, bytes_accessed=moved
        ),
    )(projected, projected, projected, halo_kv, halo_kv, attended_grad, live)


def per_device(activations, cotangent, input_weights, output_weights, key_blocks, block_counts):
    arrived = shifted(activations[0], "section", 1)
    upstream = shifted(cotangent[0], "section", -1)
    weights_in = input_weights[0]
    weights_out = output_weights[0]
    width = weights_out.shape[0]
    rows = arrived.shape[0]
    nblock = rows // BLOCK
    slot_count = key_blocks.shape[1]
    margin = REACH * BLOCK
    assert margin <= rows
    span_blocks = nblock + 2 * REACH
    first_block = lax.axis_index("seq") * nblock

    halo_rows = jnp.concatenate(
        [from_left(arrived[rows - margin :], "seq"), from_right(arrived[:margin], "seq")], axis=0
    )
    values, factor, normed = normalize(arrived)
    projected = jnp.dot(
        normed.astype(jnp.bfloat16), weights_in, preferred_element_type=jnp.float32
    ).astype(jnp.bfloat16)
    attended_grad = jnp.einsum(
        "rd,wd->rw", upstream, weights_out, preferred_element_type=jnp.float32
    ).astype(jnp.bfloat16)
    _, _, halo_normed = normalize(halo_rows)
    weights_kv = weights_in[:, width:]
    halo_kv = jnp.dot(
        halo_normed.astype(jnp.bfloat16), weights_kv, preferred_element_type=jnp.float32
    ).astype(jnp.bfloat16)

    window_index = key_blocks - first_block + REACH
    live_slots = jnp.arange(slot_count)[None, :] < block_counts[:, None]
    live_blocks = jnp.any(
        live_slots[:, :, None] & (window_index[:, :, None] == jnp.arange(span_blocks)[None, None, :]),
        axis=1,
    )
    live = jnp.where(jnp.repeat(jnp.repeat(live_blocks, BLOCK, axis=0), BLOCK, axis=1), 0.0, -1e30)

    attended, query_grad, key_grad, value_grad, halo_key_grad, halo_value_grad = attention(
        projected, halo_kv, attended_grad, live
    )
    result = (values + jnp.dot(attended, weights_out, preferred_element_type=jnp.float32)).astype(
        jnp.bfloat16
    )

    to_right = jnp.einsum(
        "rc,dc->rd",
        jnp.concatenate([halo_key_grad[margin:], halo_value_grad[margin:]], axis=1),
        weights_kv,
        preferred_element_type=jnp.float32,
    ).astype(jnp.bfloat16)
    head_part = from_left(to_right, "seq")
    to_right, halo_key_grad, halo_value_grad = lax.optimization_barrier(
        (to_right, halo_key_grad, halo_value_grad)
    )
    to_left = jnp.einsum(
        "rc,dc->rd",
        jnp.concatenate([halo_key_grad[:margin], halo_value_grad[:margin]], axis=1),
        weights_kv,
        preferred_element_type=jnp.float32,
    ).astype(jnp.bfloat16)
    tail_part = from_right(to_left, "seq")
    own_grads = jnp.concatenate([query_grad, key_grad, value_grad], axis=1)
    normed_grad = lax.optimization_barrier(
        jnp.einsum("rc,dc->rd", own_grads, weights_in, preferred_element_type=jnp.float32)
    )
    normed_grad = normed_grad + jnp.pad(head_part.astype(jnp.float32), ((0, rows - margin), (0, 0)))
    normed_grad = normed_grad + jnp.pad(tail_part.astype(jnp.float32), ((rows - margin, 0), (0, 0)))
    correction = jnp.mean(normed_grad * normed, axis=-1, keepdims=True)
    input_grad = (
        upstream.astype(jnp.float32) + factor * (normed_grad - normed * correction)
    ).astype(jnp.bfloat16)
    return (result[None], input_grad[None])


def solution(mesh):
    in_specs = (
        P("section", "seq", None),
        P("section", "seq", None),
        P("section", None, None),
        P("section", None, None),
        P("seq", None),
        P("seq"),
    )
    out_specs = (P("section", "seq", None), P("section", "seq", None))
    return jax.shard_map(
        per_device, mesh=mesh, in_specs=in_specs, out_specs=out_specs, check_vma=False
    )
```

```python
import functools

import jax
import jax.numpy as jnp
from jax import lax
from jax.experimental import pallas as pl
from jax.experimental.pallas import tpu as pltpu
from jax.sharding import PartitionSpec as P

HEAD_DIM = 128
BLOCK = 128
REACH = 2


EPSILON = 1e-05

NT = (((1,), (1,)), ((), ()))
TN = (((0,), (0,)), ((), ()))


def shifted(value, axis, steps):
    count = lax.axis_size(axis)
    pairs = [(source, (source + steps) % count) for source in range(count)]
    return lax.ppermute(value, axis, pairs)


def from_left(value, axis):
    count = lax.axis_size(axis)
    return lax.ppermute(value, axis, [(i, i + 1) for i in range(count - 1)])


def from_right(value, axis):
    count = lax.axis_size(axis)
    return lax.ppermute(value, axis, [(i + 1, i) for i in range(count - 1)])


def normalize(rows):
    values = rows.astype(jnp.float32)
    factor = lax.rsqrt(jnp.mean(values * values, axis=-1, keepdims=True) + EPSILON)
    return values, factor, values * factor


def attention_kernel(
    q_ref, ko_ref, vo_ref, kh_ref, vh_ref, do_ref, live_ref,
    out_ref, dq_ref, dk_ref, dv_ref, dkh_ref, dvh_ref,
):
    rows = q_ref.shape[0]
    margin = kh_ref.shape[0] // 2
    scaling = HEAD_DIM ** (-0.5)
    queries = q_ref[...]
    keys = jnp.concatenate([kh_ref[:margin], ko_ref[...], kh_ref[margin:]], axis=0)
    values = jnp.concatenate([vh_ref[:margin], vo_ref[...], vh_ref[margin:]], axis=0)
    grad_out = do_ref[...]
    scores = lax.dot_general(keys, queries, NT, preferred_element_type=jnp.float32) * scaling
    scores = scores + live_ref[...]
    row_max = jnp.max(scores, axis=0, keepdims=True)
    raw = jnp.exp(scores - row_max)
    weights = raw * (1.0 / jnp.sum(raw, axis=0, keepdims=True))
    weights_bf = weights.astype(jnp.bfloat16)
    out_ref[...] = lax.dot_general(
        weights_bf, values, TN, preferred_element_type=jnp.float32
    ).astype(out_ref.dtype)
    weight_grad = lax.dot_general(values, grad_out, NT, preferred_element_type=jnp.float32)
    weight_mean = jnp.sum(weights * weight_grad, axis=0, keepdims=True)
    score_grad = (weights * (weight_grad - weight_mean) * scaling).astype(jnp.bfloat16)
    dq_ref[...] = lax.dot_general(
        score_grad, keys, TN, preferred_element_type=jnp.float32
    ).astype(dq_ref.dtype)
    key_grad = jnp.dot(score_grad, queries, preferred_element_type=jnp.float32)
    value_grad = jnp.dot(weights_bf, grad_out, preferred_element_type=jnp.float32)
    dtype = dk_ref.dtype
    dk_ref[...] = key_grad[margin : margin + rows].astype(dtype)
    dv_ref[...] = value_grad[margin : margin + rows].astype(dtype)
    dkh_ref[:margin] = key_grad[:margin].astype(dtype)
    dkh_ref[margin:] = key_grad[margin + rows :].astype(dtype)
    dvh_ref[:margin] = value_grad[:margin].astype(dtype)
    dvh_ref[margin:] = value_grad[margin + rows :].astype(dtype)


def attention(projected, halo_kv, attended_grad, live):
    rows, width = attended_grad.shape
    heads = width // HEAD_DIM
    halo_rows = halo_kv.shape[0]
    window = live.shape[0]
    own = lambda offset: pl.BlockSpec((rows, HEAD_DIM), lambda h: (0, offset + h))
    side = lambda offset: pl.BlockSpec((halo_rows, HEAD_DIM), lambda h: (0, offset + h))
    flops = heads * 5 * 2 * rows * window * HEAD_DIM
    moved = 2 * (2 * projected.size + 2 * halo_kv.size + 2 * attended_grad.size) + 4 * live.size
    own_shape = jax.ShapeDtypeStruct((rows, width), jnp.bfloat16)
    side_shape = jax.ShapeDtypeStruct((halo_rows, width), jnp.bfloat16)
    return pl.pallas_call(
        attention_kernel,
        grid=(heads,),
        in_specs=[
            own(0),
            own(heads),
            own(2 * heads),
            side(0),
            side(heads),
            own(0),
            pl.BlockSpec((window, rows), lambda h: (0, 0)),
        ],
        out_specs=[own(0), own(0), own(0), own(0), side(0), side(0)],
        out_shape=[own_shape, own_shape, own_shape, own_shape, side_shape, side_shape],
        compiler_params=pltpu.CompilerParams(dimension_semantics=("arbitrary",)),
        cost_estimate=pl.CostEstimate(
            flops=flops, transcendentals=heads * rows * window, bytes_accessed=moved
        ),
    )(projected, projected, projected, halo_kv, halo_kv, attended_grad, live)


def per_device(activations, cotangent, input_weights, output_weights, key_blocks, block_counts):
    arrived = shifted(activations[0], "section", 1)
    upstream = shifted(cotangent[0], "section", -1)
    weights_in = input_weights[0]
    weights_out = output_weights[0]
    width = weights_out.shape[0]
    rows = arrived.shape[0]
    nblock = rows // BLOCK
    slot_count = key_blocks.shape[1]
    margin = REACH * BLOCK
    assert margin <= rows
    span_blocks = nblock + 2 * REACH
    first_block = lax.axis_index("seq") * nblock

    halo_rows = jnp.concatenate(
        [from_left(arrived[rows - margin :], "seq"), from_right(arrived[:margin], "seq")], axis=0
    )
    values, factor, normed = normalize(arrived)
    projected = jnp.dot(
        normed.astype(jnp.bfloat16), weights_in, preferred_element_type=jnp.float32
    ).astype(jnp.bfloat16)
    attended_grad = jnp.einsum(
        "rd,wd->rw", upstream, weights_out, preferred_element_type=jnp.float32
    ).astype(jnp.bfloat16)
    _, _, halo_normed = normalize(halo_rows)
    weights_kv = weights_in[:, width:]
    halo_kv = jnp.dot(
        halo_normed.astype(jnp.bfloat16), weights_kv, preferred_element_type=jnp.float32
    ).astype(jnp.bfloat16)

    window_index = key_blocks - first_block + REACH
    live_slots = jnp.arange(slot_count)[None, :] < block_counts[:, None]
    live_blocks = jnp.any(
        live_slots[:, :, None] & (window_index[:, :, None] == jnp.arange(span_blocks)[None, None, :]),
        axis=1,
    )
    live = jnp.where(jnp.repeat(jnp.repeat(live_blocks.T, BLOCK, axis=0), BLOCK, axis=1), 0.0, -1e30)

    attended, query_grad, key_grad, value_grad, halo_key_grad, halo_value_grad = attention(
        projected, halo_kv, attended_grad, live
    )
    result = (values + jnp.dot(attended, weights_out, preferred_element_type=jnp.float32)).astype(
        jnp.bfloat16
    )

    halo_grads = jnp.concatenate([halo_key_grad, halo_value_grad], axis=1)
    halo_normed_grad = jnp.einsum(
        "rc,dc->rd", halo_grads, weights_kv, preferred_element_type=jnp.float32
    ).astype(jnp.bfloat16)
    head_part = from_left(halo_normed_grad[margin:], "seq")
    tail_part = from_right(halo_normed_grad[:margin], "seq")
    own_grads = jnp.concatenate([query_grad, key_grad, value_grad], axis=1)
    normed_grad = lax.optimization_barrier(
        jnp.einsum("rc,dc->rd", own_grads, weights_in, preferred_element_type=jnp.float32)
    )
    normed_grad = normed_grad + jnp.pad(head_part.astype(jnp.float32), ((0, rows - margin), (0, 0)))
    normed_grad = normed_grad + jnp.pad(tail_part.astype(jnp.float32), ((rows - margin, 0), (0, 0)))
    correction = jnp.mean(normed_grad * normed, axis=-1, keepdims=True)
    input_grad = (
        upstream.astype(jnp.float32) + factor * (normed_grad - normed * correction)
    ).astype(jnp.bfloat16)
    return (result[None], input_grad[None])


def solution(mesh):
    in_specs = (
        P("section", "seq", None),
        P("section", "seq", None),
        P("section", None, None),
        P("section", None, None),
        P("seq", None),
        P("seq"),
    )
    out_specs = (P("section", "seq", None), P("section", "seq", None))
    return jax.shard_map(
        per_device, mesh=mesh, in_specs=in_specs, out_specs=out_specs, check_vma=False
    )
```

```python
import functools

import jax
import jax.numpy as jnp
from jax import lax
from jax.experimental import pallas as pl
from jax.experimental.pallas import tpu as pltpu
from jax.sharding import PartitionSpec as P

HEAD_DIM = 128
BLOCK = 128
REACH = 2


EPSILON = 1e-05

NT = (((1,), (1,)), ((), ()))
TN = (((0,), (0,)), ((), ()))


def shifted(value, axis, steps):
    count = lax.axis_size(axis)
    pairs = [(source, (source + steps) % count) for source in range(count)]
    return lax.ppermute(value, axis, pairs)


def from_left(value, axis):
    count = lax.axis_size(axis)
    return lax.ppermute(value, axis, [(i, i + 1) for i in range(count - 1)])


def from_right(value, axis):
    count = lax.axis_size(axis)
    return lax.ppermute(value, axis, [(i + 1, i) for i in range(count - 1)])


def normalize(rows):
    values = rows.astype(jnp.float32)
    factor = lax.rsqrt(jnp.mean(values * values, axis=-1, keepdims=True) + EPSILON)
    return values, factor, values * factor


GROUP = 2


def attention_kernel(
    q_ref, ko_ref, vo_ref, kh_ref, vh_ref, do_ref, live_ref,
    out_ref, dq_ref, dk_ref, dv_ref, dkh_ref, dvh_ref,
):
    rows = q_ref.shape[0]
    margin = kh_ref.shape[0] // 2
    scaling = HEAD_DIM ** (-0.5)
    live = live_ref[...]
    for part in range(q_ref.shape[1] // HEAD_DIM):
        lanes = slice(part * HEAD_DIM, (part + 1) * HEAD_DIM)
        queries = q_ref[:, lanes]
        keys = jnp.concatenate(
            [kh_ref[:margin, lanes], ko_ref[:, lanes], kh_ref[margin:, lanes]], axis=0
        )
        values = jnp.concatenate(
            [vh_ref[:margin, lanes], vo_ref[:, lanes], vh_ref[margin:, lanes]], axis=0
        )
        grad_out = do_ref[:, lanes]
        scores = lax.dot_general(queries, keys, NT, preferred_element_type=jnp.float32) * scaling
        scores = scores + live
        row_max = jnp.max(scores, axis=1, keepdims=True)
        raw = jnp.exp(scores - row_max)
        weights = raw * (1.0 / jnp.sum(raw, axis=1, keepdims=True))
        weights_bf = weights.astype(jnp.bfloat16)
        out_ref[:, lanes] = jnp.dot(
            weights_bf, values, preferred_element_type=jnp.float32
        ).astype(out_ref.dtype)
        weight_grad = lax.dot_general(grad_out, values, NT, preferred_element_type=jnp.float32)
        weight_mean = jnp.sum(weights * weight_grad, axis=1, keepdims=True)
        score_grad = (weights * (weight_grad - weight_mean) * scaling).astype(jnp.bfloat16)
        dq_ref[:, lanes] = jnp.dot(
            score_grad, keys, preferred_element_type=jnp.float32
        ).astype(dq_ref.dtype)
        key_grad = lax.dot_general(score_grad, queries, TN, preferred_element_type=jnp.float32)
        value_grad = lax.dot_general(weights_bf, grad_out, TN, preferred_element_type=jnp.float32)
        dtype = dk_ref.dtype
        dk_ref[:, lanes] = key_grad[margin : margin + rows].astype(dtype)
        dv_ref[:, lanes] = value_grad[margin : margin + rows].astype(dtype)
        dkh_ref[:margin, lanes] = key_grad[:margin].astype(dtype)
        dkh_ref[margin:, lanes] = key_grad[margin + rows :].astype(dtype)
        dvh_ref[:margin, lanes] = value_grad[:margin].astype(dtype)
        dvh_ref[margin:, lanes] = value_grad[margin + rows :].astype(dtype)


def attention(projected, halo_kv, attended_grad, live):
    rows, width = attended_grad.shape
    heads = width // HEAD_DIM
    halo_rows = halo_kv.shape[0]
    window = live.shape[1]
    group = GROUP if heads % GROUP == 0 else 1
    lanes = group * HEAD_DIM
    own = lambda offset: pl.BlockSpec((rows, lanes), lambda h: (0, offset // group + h))
    side = lambda offset: pl.BlockSpec((halo_rows, lanes), lambda h: (0, offset // group + h))
    flops = heads * 5 * 2 * rows * window * HEAD_DIM
    moved = 2 * (2 * projected.size + 2 * halo_kv.size + 2 * attended_grad.size) + 4 * live.size
    own_shape = jax.ShapeDtypeStruct((rows, width), jnp.bfloat16)
    side_shape = jax.ShapeDtypeStruct((halo_rows, width), jnp.bfloat16)
    return pl.pallas_call(
        attention_kernel,
        grid=(heads // group,),
        in_specs=[
            own(0),
            own(heads),
            own(2 * heads),
            side(0),
            side(heads),
            own(0),
            pl.BlockSpec((rows, window), lambda h: (0, 0)),
        ],
        out_specs=[own(0), own(0), own(0), own(0), side(0), side(0)],
        out_shape=[own_shape, own_shape, own_shape, own_shape, side_shape, side_shape],
        compiler_params=pltpu.CompilerParams(dimension_semantics=("arbitrary",)),
        cost_estimate=pl.CostEstimate(
            flops=flops, transcendentals=heads * rows * window, bytes_accessed=moved
        ),
    )(projected, projected, projected, halo_kv, halo_kv, attended_grad, live)


def per_device(activations, cotangent, input_weights, output_weights, key_blocks, block_counts):
    arrived = shifted(activations[0], "section", 1)
    upstream = shifted(cotangent[0], "section", -1)
    weights_in = input_weights[0]
    weights_out = output_weights[0]
    width = weights_out.shape[0]
    rows = arrived.shape[0]
    nblock = rows // BLOCK
    slot_count = key_blocks.shape[1]
    margin = REACH * BLOCK
    assert margin <= rows
    span_blocks = nblock + 2 * REACH
    first_block = lax.axis_index("seq") * nblock

    halo_rows = jnp.concatenate(
        [from_left(arrived[rows - margin :], "seq"), from_right(arrived[:margin], "seq")], axis=0
    )
    values, factor, normed = normalize(arrived)
    projected = jnp.dot(
        normed.astype(jnp.bfloat16), weights_in, preferred_element_type=jnp.float32
    ).astype(jnp.bfloat16)
    attended_grad = jnp.einsum(
        "rd,wd->rw", upstream, weights_out, preferred_element_type=jnp.float32
    ).astype(jnp.bfloat16)
    _, _, halo_normed = normalize(halo_rows)
    weights_kv = weights_in[:, width:]
    halo_kv = jnp.dot(
        halo_normed.astype(jnp.bfloat16), weights_kv, preferred_element_type=jnp.float32
    ).astype(jnp.bfloat16)

    window_index = key_blocks - first_block + REACH
    live_slots = jnp.arange(slot_count)[None, :] < block_counts[:, None]
    live_blocks = jnp.any(
        live_slots[:, :, None] & (window_index[:, :, None] == jnp.arange(span_blocks)[None, None, :]),
        axis=1,
    )
    live = jnp.where(jnp.repeat(jnp.repeat(live_blocks, BLOCK, axis=0), BLOCK, axis=1), 0.0, -1e30)

    attended, query_grad, key_grad, value_grad, halo_key_grad, halo_value_grad = attention(
        projected, halo_kv, attended_grad, live
    )
    result = (values + jnp.dot(attended, weights_out, preferred_element_type=jnp.float32)).astype(
        jnp.bfloat16
    )

    halo_grads = jnp.concatenate([halo_key_grad, halo_value_grad], axis=1)
    halo_normed_grad = jnp.einsum(
        "rc,dc->rd", halo_grads, weights_kv, preferred_element_type=jnp.float32
    ).astype(jnp.bfloat16)
    head_part = from_left(halo_normed_grad[margin:], "seq")
    tail_part = from_right(halo_normed_grad[:margin], "seq")
    own_grads = jnp.concatenate([query_grad, key_grad, value_grad], axis=1)
    normed_grad = lax.optimization_barrier(
        jnp.einsum("rc,dc->rd", own_grads, weights_in, preferred_element_type=jnp.float32)
    )
    normed_grad = normed_grad + jnp.pad(head_part.astype(jnp.float32), ((0, rows - margin), (0, 0)))
    normed_grad = normed_grad + jnp.pad(tail_part.astype(jnp.float32), ((rows - margin, 0), (0, 0)))
    correction = jnp.mean(normed_grad * normed, axis=-1, keepdims=True)
    input_grad = (
        upstream.astype(jnp.float32) + factor * (normed_grad - normed * correction)
    ).astype(jnp.bfloat16)
    return (result[None], input_grad[None])


def solution(mesh):
    in_specs = (
        P("section", "seq", None),
        P("section", "seq", None),
        P("section", None, None),
        P("section", None, None),
        P("seq", None),
        P("seq"),
    )
    out_specs = (P("section", "seq", None), P("section", "seq", None))
    return jax.shard_map(
        per_device, mesh=mesh, in_specs=in_specs, out_specs=out_specs, check_vma=False
    )
```

```python
import functools

import jax
import jax.numpy as jnp
from jax import lax
from jax.experimental import pallas as pl
from jax.experimental.pallas import tpu as pltpu
from jax.sharding import PartitionSpec as P

HEAD_DIM = 128
BLOCK = 128
REACH = 2


EPSILON = 1e-05

NT = (((1,), (1,)), ((), ()))
TN = (((0,), (0,)), ((), ()))


def shifted(value, axis, steps):
    count = lax.axis_size(axis)
    pairs = [(source, (source + steps) % count) for source in range(count)]
    return lax.ppermute(value, axis, pairs)


def from_left(value, axis):
    count = lax.axis_size(axis)
    return lax.ppermute(value, axis, [(i, i + 1) for i in range(count - 1)])


def from_right(value, axis):
    count = lax.axis_size(axis)
    return lax.ppermute(value, axis, [(i + 1, i) for i in range(count - 1)])


def normalize(rows):
    values = rows.astype(jnp.float32)
    factor = lax.rsqrt(jnp.mean(values * values, axis=-1, keepdims=True) + EPSILON)
    return values, factor, values * factor


GROUP = 4


def attention_kernel(
    q_ref, ko_ref, vo_ref, kh_ref, vh_ref, do_ref, live_ref,
    out_ref, dq_ref, dk_ref, dv_ref, dkh_ref, dvh_ref,
):
    rows = q_ref.shape[0]
    margin = kh_ref.shape[0] // 2
    scaling = HEAD_DIM ** (-0.5)
    live = live_ref[...]
    for part in range(q_ref.shape[1] // HEAD_DIM):
        lanes = slice(part * HEAD_DIM, (part + 1) * HEAD_DIM)
        queries = q_ref[:, lanes]
        keys = jnp.concatenate(
            [kh_ref[:margin, lanes], ko_ref[:, lanes], kh_ref[margin:, lanes]], axis=0
        )
        values = jnp.concatenate(
            [vh_ref[:margin, lanes], vo_ref[:, lanes], vh_ref[margin:, lanes]], axis=0
        )
        grad_out = do_ref[:, lanes]
        scores = lax.dot_general(queries, keys, NT, preferred_element_type=jnp.float32) * scaling
        scores = scores + live
        row_max = jnp.max(scores, axis=1, keepdims=True)
        raw = jnp.exp(scores - row_max)
        weights = raw * (1.0 / jnp.sum(raw, axis=1, keepdims=True))
        weights_bf = weights.astype(jnp.bfloat16)
        out_ref[:, lanes] = jnp.dot(
            weights_bf, values, preferred_element_type=jnp.float32
        ).astype(out_ref.dtype)
        weight_grad = lax.dot_general(grad_out, values, NT, preferred_element_type=jnp.float32)
        weight_mean = jnp.sum(weights * weight_grad, axis=1, keepdims=True)
        score_grad = (weights * (weight_grad - weight_mean) * scaling).astype(jnp.bfloat16)
        dq_ref[:, lanes] = jnp.dot(
            score_grad, keys, preferred_element_type=jnp.float32
        ).astype(dq_ref.dtype)
        key_grad = lax.dot_general(score_grad, queries, TN, preferred_element_type=jnp.float32)
        value_grad = lax.dot_general(weights_bf, grad_out, TN, preferred_element_type=jnp.float32)
        dtype = dk_ref.dtype
        dk_ref[:, lanes] = key_grad[margin : margin + rows].astype(dtype)
        dv_ref[:, lanes] = value_grad[margin : margin + rows].astype(dtype)
        dkh_ref[:margin, lanes] = key_grad[:margin].astype(dtype)
        dkh_ref[margin:, lanes] = key_grad[margin + rows :].astype(dtype)
        dvh_ref[:margin, lanes] = value_grad[:margin].astype(dtype)
        dvh_ref[margin:, lanes] = value_grad[margin + rows :].astype(dtype)


def attention(projected, halo_kv, attended_grad, live):
    rows, width = attended_grad.shape
    heads = width // HEAD_DIM
    halo_rows = halo_kv.shape[0]
    window = live.shape[1]
    group = GROUP if heads % GROUP == 0 else 1
    lanes = group * HEAD_DIM
    own = lambda offset: pl.BlockSpec((rows, lanes), lambda h: (0, offset // group + h))
    side = lambda offset: pl.BlockSpec((halo_rows, lanes), lambda h: (0, offset // group + h))
    flops = heads * 5 * 2 * rows * window * HEAD_DIM
    moved = 2 * (2 * projected.size + 2 * halo_kv.size + 2 * attended_grad.size) + 4 * live.size
    own_shape = jax.ShapeDtypeStruct((rows, width), jnp.bfloat16)
    side_shape = jax.ShapeDtypeStruct((halo_rows, width), jnp.bfloat16)
    return pl.pallas_call(
        attention_kernel,
        grid=(heads // group,),
        in_specs=[
            own(0),
            own(heads),
            own(2 * heads),
            side(0),
            side(heads),
            own(0),
            pl.BlockSpec((rows, window), lambda h: (0, 0)),
        ],
        out_specs=[own(0), own(0), own(0), own(0), side(0), side(0)],
        out_shape=[own_shape, own_shape, own_shape, own_shape, side_shape, side_shape],
        compiler_params=pltpu.CompilerParams(dimension_semantics=("arbitrary",)),
        cost_estimate=pl.CostEstimate(
            flops=flops, transcendentals=heads * rows * window, bytes_accessed=moved
        ),
    )(projected, projected, projected, halo_kv, halo_kv, attended_grad, live)


def per_device(activations, cotangent, input_weights, output_weights, key_blocks, block_counts):
    arrived = shifted(activations[0], "section", 1)
    upstream = shifted(cotangent[0], "section", -1)
    weights_in = input_weights[0]
    weights_out = output_weights[0]
    width = weights_out.shape[0]
    rows = arrived.shape[0]
    nblock = rows // BLOCK
    slot_count = key_blocks.shape[1]
    margin = REACH * BLOCK
    assert margin <= rows
    span_blocks = nblock + 2 * REACH
    first_block = lax.axis_index("seq") * nblock

    halo_rows = jnp.concatenate(
        [from_left(arrived[rows - margin :], "seq"), from_right(arrived[:margin], "seq")], axis=0
    )
    values, factor, normed = normalize(arrived)
    projected = jnp.dot(
        normed.astype(jnp.bfloat16), weights_in, preferred_element_type=jnp.float32
    ).astype(jnp.bfloat16)
    attended_grad = jnp.einsum(
        "rd,wd->rw", upstream, weights_out, preferred_element_type=jnp.float32
    ).astype(jnp.bfloat16)
    _, _, halo_normed = normalize(halo_rows)
    weights_kv = weights_in[:, width:]
    halo_kv = jnp.dot(
        halo_normed.astype(jnp.bfloat16), weights_kv, preferred_element_type=jnp.float32
    ).astype(jnp.bfloat16)

    window_index = key_blocks - first_block + REACH
    live_slots = jnp.arange(slot_count)[None, :] < block_counts[:, None]
    live_blocks = jnp.any(
        live_slots[:, :, None] & (window_index[:, :, None] == jnp.arange(span_blocks)[None, None, :]),
        axis=1,
    )
    live = jnp.where(jnp.repeat(jnp.repeat(live_blocks, BLOCK, axis=0), BLOCK, axis=1), 0.0, -1e30)

    attended, query_grad, key_grad, value_grad, halo_key_grad, halo_value_grad = attention(
        projected, halo_kv, attended_grad, live
    )
    result = (values + jnp.dot(attended, weights_out, preferred_element_type=jnp.float32)).astype(
        jnp.bfloat16
    )

    halo_grads = jnp.concatenate([halo_key_grad, halo_value_grad], axis=1)
    halo_normed_grad = jnp.einsum(
        "rc,dc->rd", halo_grads, weights_kv, preferred_element_type=jnp.float32
    ).astype(jnp.bfloat16)
    head_part = from_left(halo_normed_grad[margin:], "seq")
    tail_part = from_right(halo_normed_grad[:margin], "seq")
    own_grads = jnp.concatenate([query_grad, key_grad, value_grad], axis=1)
    normed_grad = lax.optimization_barrier(
        jnp.einsum("rc,dc->rd", own_grads, weights_in, preferred_element_type=jnp.float32)
    )
    normed_grad = normed_grad + jnp.pad(head_part.astype(jnp.float32), ((0, rows - margin), (0, 0)))
    normed_grad = normed_grad + jnp.pad(tail_part.astype(jnp.float32), ((rows - margin, 0), (0, 0)))
    correction = jnp.mean(normed_grad * normed, axis=-1, keepdims=True)
    input_grad = (
        upstream.astype(jnp.float32) + factor * (normed_grad - normed * correction)
    ).astype(jnp.bfloat16)
    return (result[None], input_grad[None])


def solution(mesh):
    in_specs = (
        P("section", "seq", None),
        P("section", "seq", None),
        P("section", None, None),
        P("section", None, None),
        P("seq", None),
        P("seq"),
    )
    out_specs = (P("section", "seq", None), P("section", "seq", None))
    return jax.shard_map(
        per_device, mesh=mesh, in_specs=in_specs, out_specs=out_specs, check_vma=False
    )
```

```python
import functools

import jax
import jax.numpy as jnp
from jax import lax
from jax.experimental import pallas as pl
from jax.experimental.pallas import tpu as pltpu
from jax.sharding import PartitionSpec as P

HEAD_DIM = 128
BLOCK = 128
REACH = 2


EPSILON = 1e-05

NT = (((1,), (1,)), ((), ()))
TN = (((0,), (0,)), ((), ()))


def shifted(value, axis, steps):
    count = lax.axis_size(axis)
    pairs = [(source, (source + steps) % count) for source in range(count)]
    return lax.ppermute(value, axis, pairs)


def from_left(value, axis):
    count = lax.axis_size(axis)
    return lax.ppermute(value, axis, [(i, i + 1) for i in range(count - 1)])


def from_right(value, axis):
    count = lax.axis_size(axis)
    return lax.ppermute(value, axis, [(i + 1, i) for i in range(count - 1)])


def normalize(rows):
    values = rows.astype(jnp.float32)
    factor = lax.rsqrt(jnp.mean(values * values, axis=-1, keepdims=True) + EPSILON)
    return values, factor, values * factor


GROUP = 2


def attention_kernel(
    q_ref, ko_ref, vo_ref, kl_ref, vl_ref, kr_ref, vr_ref, do_ref, live_ref,
    out_ref, dq_ref, dk_ref, dv_ref, dkh_ref, dvh_ref,
):
    rows = q_ref.shape[0]
    margin = kl_ref.shape[0]
    scaling = HEAD_DIM ** (-0.5)
    live = live_ref[...]
    for part in range(q_ref.shape[1] // HEAD_DIM):
        lanes = slice(part * HEAD_DIM, (part + 1) * HEAD_DIM)
        queries = q_ref[:, lanes]
        keys = jnp.concatenate(
            [kl_ref[:, lanes], ko_ref[:, lanes], kr_ref[:, lanes]], axis=0
        )
        values = jnp.concatenate(
            [vl_ref[:, lanes], vo_ref[:, lanes], vr_ref[:, lanes]], axis=0
        )
        grad_out = do_ref[:, lanes]
        scores = lax.dot_general(queries, keys, NT, preferred_element_type=jnp.float32) * scaling
        scores = scores + live
        row_max = jnp.max(scores, axis=1, keepdims=True)
        raw = jnp.exp(scores - row_max)
        weights = raw * (1.0 / jnp.sum(raw, axis=1, keepdims=True))
        weights_bf = weights.astype(jnp.bfloat16)
        out_ref[:, lanes] = jnp.dot(
            weights_bf, values, preferred_element_type=jnp.float32
        ).astype(out_ref.dtype)
        weight_grad = lax.dot_general(grad_out, values, NT, preferred_element_type=jnp.float32)
        weight_mean = jnp.sum(weights * weight_grad, axis=1, keepdims=True)
        score_grad = (weights * (weight_grad - weight_mean) * scaling).astype(jnp.bfloat16)
        dq_ref[:, lanes] = jnp.dot(
            score_grad, keys, preferred_element_type=jnp.float32
        ).astype(dq_ref.dtype)
        key_grad = lax.dot_general(score_grad, queries, TN, preferred_element_type=jnp.float32)
        value_grad = lax.dot_general(weights_bf, grad_out, TN, preferred_element_type=jnp.float32)
        dtype = dk_ref.dtype
        dk_ref[:, lanes] = key_grad[margin : margin + rows].astype(dtype)
        dv_ref[:, lanes] = value_grad[margin : margin + rows].astype(dtype)
        dkh_ref[:margin, lanes] = key_grad[:margin].astype(dtype)
        dkh_ref[margin:, lanes] = key_grad[margin + rows :].astype(dtype)
        dvh_ref[:margin, lanes] = value_grad[:margin].astype(dtype)
        dvh_ref[margin:, lanes] = value_grad[margin + rows :].astype(dtype)


def attention(projected, left_kv, right_kv, attended_grad, live):
    rows, width = attended_grad.shape
    heads = width // HEAD_DIM
    margin = left_kv.shape[0]
    halo_rows = 2 * margin
    window = live.shape[1]
    group = GROUP if heads % GROUP == 0 else 1
    lanes = group * HEAD_DIM
    own = lambda offset: pl.BlockSpec((rows, lanes), lambda h: (0, offset // group + h))
    side = lambda offset: pl.BlockSpec((halo_rows, lanes), lambda h: (0, offset // group + h))
    edge = lambda offset: pl.BlockSpec((margin, lanes), lambda h: (0, offset // group + h))
    flops = heads * 5 * 2 * rows * window * HEAD_DIM
    moved = 2 * (2 * projected.size + 4 * left_kv.size + 2 * attended_grad.size) + 4 * live.size
    own_shape = jax.ShapeDtypeStruct((rows, width), jnp.bfloat16)
    side_shape = jax.ShapeDtypeStruct((halo_rows, width), jnp.bfloat16)
    return pl.pallas_call(
        attention_kernel,
        grid=(heads // group,),
        in_specs=[
            own(0),
            own(heads),
            own(2 * heads),
            edge(0),
            edge(heads),
            edge(0),
            edge(heads),
            own(0),
            pl.BlockSpec((rows, window), lambda h: (0, 0)),
        ],
        out_specs=[own(0), own(0), own(0), own(0), side(0), side(0)],
        out_shape=[own_shape, own_shape, own_shape, own_shape, side_shape, side_shape],
        compiler_params=pltpu.CompilerParams(dimension_semantics=("arbitrary",)),
        cost_estimate=pl.CostEstimate(
            flops=flops, transcendentals=heads * rows * window, bytes_accessed=moved
        ),
    )(
        projected, projected, projected, left_kv, left_kv, right_kv, right_kv, attended_grad, live
    )


def per_device(activations, cotangent, input_weights, output_weights, key_blocks, block_counts):
    arrived = shifted(activations[0], "section", 1)
    upstream = shifted(cotangent[0], "section", -1)
    weights_in = input_weights[0]
    weights_out = output_weights[0]
    width = weights_out.shape[0]
    rows = arrived.shape[0]
    nblock = rows // BLOCK
    slot_count = key_blocks.shape[1]
    margin = REACH * BLOCK
    assert margin <= rows
    span_blocks = nblock + 2 * REACH
    first_block = lax.axis_index("seq") * nblock

    left_rows = from_left(arrived[rows - margin :], "seq")
    right_rows = from_right(arrived[:margin], "seq")
    values, factor, normed = normalize(arrived)
    projected = jnp.dot(
        normed.astype(jnp.bfloat16), weights_in, preferred_element_type=jnp.float32
    ).astype(jnp.bfloat16)
    attended_grad = jnp.einsum(
        "rd,wd->rw", upstream, weights_out, preferred_element_type=jnp.float32
    ).astype(jnp.bfloat16)
    weights_kv = weights_in[:, width:]

    def side_kv(side_rows):
        _, _, side_normed = normalize(side_rows)
        return jnp.dot(
            side_normed.astype(jnp.bfloat16), weights_kv, preferred_element_type=jnp.float32
        ).astype(jnp.bfloat16)

    right_kv = side_kv(right_rows)
    right_kv, left_rows = lax.optimization_barrier((right_kv, left_rows))
    left_kv = side_kv(left_rows)

    window_index = key_blocks - first_block + REACH
    live_slots = jnp.arange(slot_count)[None, :] < block_counts[:, None]
    live_blocks = jnp.any(
        live_slots[:, :, None] & (window_index[:, :, None] == jnp.arange(span_blocks)[None, None, :]),
        axis=1,
    )
    live = jnp.where(jnp.repeat(jnp.repeat(live_blocks, BLOCK, axis=0), BLOCK, axis=1), 0.0, -1e30)

    attended, query_grad, key_grad, value_grad, halo_key_grad, halo_value_grad = attention(
        projected, left_kv, right_kv, attended_grad, live
    )
    result = (values + jnp.dot(attended, weights_out, preferred_element_type=jnp.float32)).astype(
        jnp.bfloat16
    )

    halo_grads = jnp.concatenate([halo_key_grad, halo_value_grad], axis=1)
    halo_normed_grad = jnp.einsum(
        "rc,dc->rd", halo_grads, weights_kv, preferred_element_type=jnp.float32
    ).astype(jnp.bfloat16)
    head_part = from_left(halo_normed_grad[margin:], "seq")
    tail_part = from_right(halo_normed_grad[:margin], "seq")
    own_grads = jnp.concatenate([query_grad, key_grad, value_grad], axis=1)
    normed_grad = lax.optimization_barrier(
        jnp.einsum("rc,dc->rd", own_grads, weights_in, preferred_element_type=jnp.float32)
    )
    normed_grad = normed_grad + jnp.pad(head_part.astype(jnp.float32), ((0, rows - margin), (0, 0)))
    normed_grad = normed_grad + jnp.pad(tail_part.astype(jnp.float32), ((rows - margin, 0), (0, 0)))
    correction = jnp.mean(normed_grad * normed, axis=-1, keepdims=True)
    input_grad = (
        upstream.astype(jnp.float32) + factor * (normed_grad - normed * correction)
    ).astype(jnp.bfloat16)
    return (result[None], input_grad[None])


def solution(mesh):
    in_specs = (
        P("section", "seq", None),
        P("section", "seq", None),
        P("section", None, None),
        P("section", None, None),
        P("seq", None),
        P("seq"),
    )
    out_specs = (P("section", "seq", None), P("section", "seq", None))
    return jax.shard_map(
        per_device, mesh=mesh, in_specs=in_specs, out_specs=out_specs, check_vma=False
    )
```

```python
import functools

import jax
import jax.numpy as jnp
from jax import lax
from jax.experimental import pallas as pl
from jax.experimental.pallas import tpu as pltpu
from jax.sharding import PartitionSpec as P

HEAD_DIM = 128
BLOCK = 128
REACH = 2


EPSILON = 1e-05

NT = (((1,), (1,)), ((), ()))
TN = (((0,), (0,)), ((), ()))


def shifted(value, axis, steps):
    count = lax.axis_size(axis)
    pairs = [(source, (source + steps) % count) for source in range(count)]
    return lax.ppermute(value, axis, pairs)


def from_left(value, axis):
    count = lax.axis_size(axis)
    return lax.ppermute(value, axis, [(i, i + 1) for i in range(count - 1)])


def from_right(value, axis):
    count = lax.axis_size(axis)
    return lax.ppermute(value, axis, [(i + 1, i) for i in range(count - 1)])


def normalize(rows):
    values = rows.astype(jnp.float32)
    factor = lax.rsqrt(jnp.mean(values * values, axis=-1, keepdims=True) + EPSILON)
    return values, factor, values * factor


GROUP = 2


def attention_kernel(
    q_ref, ko_ref, vo_ref, kl_ref, vl_ref, kr_ref, vr_ref, do_ref, live_ref,
    out_ref, dq_ref, dk_ref, dv_ref, dkh_ref, dvh_ref,
):
    rows = q_ref.shape[0]
    margin = kl_ref.shape[0]
    scaling = HEAD_DIM ** (-0.5)
    live = live_ref[...]
    for part in range(q_ref.shape[1] // HEAD_DIM):
        lanes = slice(part * HEAD_DIM, (part + 1) * HEAD_DIM)
        queries = q_ref[:, lanes]
        keys = jnp.concatenate(
            [kl_ref[:, lanes], ko_ref[:, lanes], kr_ref[:, lanes]], axis=0
        )
        values = jnp.concatenate(
            [vl_ref[:, lanes], vo_ref[:, lanes], vr_ref[:, lanes]], axis=0
        )
        grad_out = do_ref[:, lanes]
        scores = lax.dot_general(queries, keys, NT, preferred_element_type=jnp.float32) * scaling
        scores = scores + live
        row_max = jnp.max(scores, axis=1, keepdims=True)
        raw = jnp.exp(scores - row_max)
        weights = raw * (1.0 / jnp.sum(raw, axis=1, keepdims=True))
        weights_bf = weights.astype(jnp.bfloat16)
        out_ref[:, lanes] = jnp.dot(
            weights_bf, values, preferred_element_type=jnp.float32
        ).astype(out_ref.dtype)
        weight_grad = lax.dot_general(grad_out, values, NT, preferred_element_type=jnp.float32)
        weight_mean = jnp.sum(weights * weight_grad, axis=1, keepdims=True)
        score_grad = (weights * (weight_grad - weight_mean) * scaling).astype(jnp.bfloat16)
        dq_ref[:, lanes] = jnp.dot(
            score_grad, keys, preferred_element_type=jnp.float32
        ).astype(dq_ref.dtype)
        key_grad = lax.dot_general(score_grad, queries, TN, preferred_element_type=jnp.float32)
        value_grad = lax.dot_general(weights_bf, grad_out, TN, preferred_element_type=jnp.float32)
        dtype = dk_ref.dtype
        dk_ref[:, lanes] = key_grad[margin : margin + rows].astype(dtype)
        dv_ref[:, lanes] = value_grad[margin : margin + rows].astype(dtype)
        dkh_ref[:margin, lanes] = key_grad[:margin].astype(dtype)
        dkh_ref[margin:, lanes] = key_grad[margin + rows :].astype(dtype)
        dvh_ref[:margin, lanes] = value_grad[:margin].astype(dtype)
        dvh_ref[margin:, lanes] = value_grad[margin + rows :].astype(dtype)


def attention(projected, left_kv, right_kv, attended_grad, live):
    rows, width = attended_grad.shape
    heads = width // HEAD_DIM
    margin = left_kv.shape[0]
    halo_rows = 2 * margin
    window = live.shape[1]
    group = GROUP if heads % GROUP == 0 else 1
    lanes = group * HEAD_DIM
    own = lambda offset: pl.BlockSpec((rows, lanes), lambda h: (0, offset // group + h))
    side = lambda offset: pl.BlockSpec((halo_rows, lanes), lambda h: (0, offset // group + h))
    edge = lambda offset: pl.BlockSpec((margin, lanes), lambda h: (0, offset // group + h))
    flops = heads * 5 * 2 * rows * window * HEAD_DIM
    moved = 2 * (2 * projected.size + 4 * left_kv.size + 2 * attended_grad.size) + 4 * live.size
    own_shape = jax.ShapeDtypeStruct((rows, width), jnp.bfloat16)
    side_shape = jax.ShapeDtypeStruct((halo_rows, width), jnp.bfloat16)
    return pl.pallas_call(
        attention_kernel,
        grid=(heads // group,),
        in_specs=[
            own(0),
            own(heads),
            own(2 * heads),
            edge(0),
            edge(heads),
            edge(0),
            edge(heads),
            own(0),
            pl.BlockSpec((rows, window), lambda h: (0, 0)),
        ],
        out_specs=[own(0), own(0), own(0), own(0), side(0), side(0)],
        out_shape=[own_shape, own_shape, own_shape, own_shape, side_shape, side_shape],
        compiler_params=pltpu.CompilerParams(dimension_semantics=("arbitrary",)),
        cost_estimate=pl.CostEstimate(
            flops=flops, transcendentals=heads * rows * window, bytes_accessed=moved
        ),
    )(
        projected, projected, projected, left_kv, left_kv, right_kv, right_kv, attended_grad, live
    )


def per_device(activations, cotangent, input_weights, output_weights, key_blocks, block_counts):
    arrived = shifted(activations[0], "section", 1)
    upstream = shifted(cotangent[0], "section", -1)
    weights_in = input_weights[0]
    weights_out = output_weights[0]
    width = weights_out.shape[0]
    rows = arrived.shape[0]
    nblock = rows // BLOCK
    slot_count = key_blocks.shape[1]
    margin = REACH * BLOCK
    assert margin <= rows
    span_blocks = nblock + 2 * REACH
    first_block = lax.axis_index("seq") * nblock

    left_rows = from_left(arrived[rows - margin :], "seq")
    right_rows = from_right(arrived[:margin], "seq")
    values, factor, normed = normalize(arrived)
    projected = jnp.dot(
        normed.astype(jnp.bfloat16), weights_in, preferred_element_type=jnp.float32
    ).astype(jnp.bfloat16)
    attended_grad = jnp.einsum(
        "rd,wd->rw", upstream, weights_out, preferred_element_type=jnp.float32
    ).astype(jnp.bfloat16)
    weights_kv = weights_in[:, width:]

    def side_kv(side_rows):
        _, _, side_normed = normalize(side_rows)
        return jnp.dot(
            side_normed.astype(jnp.bfloat16), weights_kv, preferred_element_type=jnp.float32
        ).astype(jnp.bfloat16)

    left_kv = side_kv(left_rows)
    left_kv, right_rows = lax.optimization_barrier((left_kv, right_rows))
    right_kv = side_kv(right_rows)

    window_index = key_blocks - first_block + REACH
    live_slots = jnp.arange(slot_count)[None, :] < block_counts[:, None]
    live_blocks = jnp.any(
        live_slots[:, :, None] & (window_index[:, :, None] == jnp.arange(span_blocks)[None, None, :]),
        axis=1,
    )
    live = jnp.where(jnp.repeat(jnp.repeat(live_blocks, BLOCK, axis=0), BLOCK, axis=1), 0.0, -1e30)

    attended, query_grad, key_grad, value_grad, halo_key_grad, halo_value_grad = attention(
        projected, left_kv, right_kv, attended_grad, live
    )
    result = (values + jnp.dot(attended, weights_out, preferred_element_type=jnp.float32)).astype(
        jnp.bfloat16
    )

    halo_grads = jnp.concatenate([halo_key_grad, halo_value_grad], axis=1)
    halo_normed_grad = jnp.einsum(
        "rc,dc->rd", halo_grads, weights_kv, preferred_element_type=jnp.float32
    ).astype(jnp.bfloat16)
    head_part = from_left(halo_normed_grad[margin:], "seq")
    tail_part = from_right(halo_normed_grad[:margin], "seq")
    own_grads = jnp.concatenate([query_grad, key_grad, value_grad], axis=1)
    normed_grad = lax.optimization_barrier(
        jnp.einsum("rc,dc->rd", own_grads, weights_in, preferred_element_type=jnp.float32)
    )
    normed_grad = normed_grad + jnp.pad(head_part.astype(jnp.float32), ((0, rows - margin), (0, 0)))
    normed_grad = normed_grad + jnp.pad(tail_part.astype(jnp.float32), ((rows - margin, 0), (0, 0)))
    correction = jnp.mean(normed_grad * normed, axis=-1, keepdims=True)
    input_grad = (
        upstream.astype(jnp.float32) + factor * (normed_grad - normed * correction)
    ).astype(jnp.bfloat16)
    return (result[None], input_grad[None])


def solution(mesh):
    in_specs = (
        P("section", "seq", None),
        P("section", "seq", None),
        P("section", None, None),
        P("section", None, None),
        P("seq", None),
        P("seq"),
    )
    out_specs = (P("section", "seq", None), P("section", "seq", None))
    return jax.shard_map(
        per_device, mesh=mesh, in_specs=in_specs, out_specs=out_specs, check_vma=False
    )
```
